256 devices in a mesh: segment: 2 (over core), ctx: 64 (over x, z, y_hi), tp: 2 (over y_lo).
Axes of the slice: x: 4, y: 4 (y_hi: 2, y_lo: 2; y = y_hi * 2 + y_lo), z: 8, core: 2. Of those that a mesh axis runs over, the one named last changes fastest.
Arguments:
- queries: bfloat16 [8192, 32, 128], P('ctx', 'tp'), may hold values from -14 to 14
- keys: bfloat16 [8192, 8, 128], P('ctx', 'tp'), may hold values from -10 to 10
- values: bfloat16 [8192, 8, 128], P('ctx', 'tp'), may hold values from -6 to 6
- layer_in: bfloat16 [8192, 4096], P('ctx', 'tp'), may hold values from -6 to 6
- w_bc: bfloat16 [1, 4096, 1024], P(None, 'tp'), may hold values from -0.09375 to 0.09375
- w_dt: bfloat16 [1, 4096, 64], P(None, 'tp'), may hold values from -0.09375 to 0.09375
- dt_bias: float32 [1, 64], P(None, 'tp'), may hold values from -1 to 1
- decay_rate: float32 [1, 64], P(None, 'tp'), may hold values from 1.2207031e-05 to 0.06
- skip_gain: float32 [1, 64], P(None, 'tp'), may hold values from 0.5 to 2
- out_gain: float32 [1, 64, 64], P(None, 'tp'), may hold values from 0.5 to 1.5
Outputs:
- section_out: bfloat16 [2, 8192, 4096], P('segment', 'ctx', 'tp')
The draws below stay inside these ranges and needn't reach their ends.
All inputs are finite; a program needn't handle non-finite values.
Results may differ from the reference program's by a relative error of at most 0.002.
Values may be sent and summed in bfloat16 or wider, within the bound.
No kernel may reach another device: no remote copies, remote signals or barrier semaphores. Data moves between devices by JAX's collectives and lax.ppermute only.
A program may use at most 256 MiB of HBM per device.

```python
import math
import jax
import jax.numpy as jnp
from jax import lax

QHEADS = 32
KVHEADS = 8
HEAD = 128
SHEADS = 64
SHEAD = 64
GROUPS = 4
STATE = 128
LAYERS = 1
L_DEV = 128
SEQ = 8192


def draw_queries(key, part):
    shape_all = (SEQ, QHEADS, HEAD)
    return jnp.clip(1.7 * jax.random.normal(jax.random.fold_in(key, 1), shape_all, jnp.float32), -10.0, 10.0).astype(jnp.bfloat16)


def draw_keys(key, part):
    shape_all = (SEQ, KVHEADS, HEAD)
    return jnp.clip(1.7 * jax.random.normal(jax.random.fold_in(key, 2), shape_all, jnp.float32), -10.0, 10.0).astype(jnp.bfloat16)


def draw_decay_rate(key, part):
    shape_all = (LAYERS, SHEADS)
    pick_draw = jax.random.uniform(jax.random.fold_in(key, 1), shape_all, jnp.float32)
    slow_rate = jnp.exp(jax.random.uniform(jax.random.fold_in(key, 2), shape_all, jnp.float32, jnp.log(0.1), 0.0)) / SEQ
    fast_rate = jnp.exp(jax.random.uniform(jax.random.fold_in(key, 3), shape_all, jnp.float32, jnp.log(0.02), jnp.log(0.06)))
    slow_share = 0.5
    return jnp.where(pick_draw < slow_share, slow_rate, fast_rate)


def block_scale(rng, extent, shards, least, top_value):
    gain = 1.0
    for axis_at, shards_of in shards:
        steps = jax.random.uniform(jax.random.fold_in(jax.random.fold_in(rng, 6), axis_at), (shards_of,), jnp.float32, least / len(shards), top_value / len(shards))
        gain = gain * jnp.repeat(jnp.exp(steps), extent[axis_at] // shards_of).reshape((-1,) + (1,) * (len(extent) - 1 - axis_at))
    return gain


def normal_values(own_key, shape, scale, most, split=(), kind=jnp.bfloat16):
    values = jax.random.normal(own_key, shape, jnp.float32) * scale
    if len(split) > 0:
        values = block_scale(own_key, shape, split, -0.22, 0.18) * values
    return jnp.clip(values, min=-most, max=most).astype(kind)


def setup_inputs(seed: int = 0) -> dict:
    seeds = jax.random.split(jax.random.key(seed), 11)
    queries = draw_queries(jax.random.fold_in(seeds[10], 71), 0)
    keys = draw_keys(jax.random.fold_in(seeds[10], 71), 0)
    values = normal_values(seeds[2], (SEQ, KVHEADS, HEAD), 1.0, 6.0, ((0, 64), (1, 2)))
    layer_in = normal_values(seeds[3], (SEQ, SHEADS * SHEAD), 1.0, 6.0, ((0, 64), (1, 2)))
    w_bc = normal_values(seeds[4], (LAYERS, SHEADS * SHEAD, 2 * GROUPS * STATE), (SHEADS * SHEAD) ** -0.5, 0.09375, ((1, 2),))
    w_dt = normal_values(seeds[5], (LAYERS, SHEADS * SHEAD, SHEADS), (SHEADS * SHEAD) ** -0.5, 0.09375, ((1, 2),))
    dt_bias = jnp.clip(jax.random.uniform(seeds[6], (LAYERS, SHEADS), jnp.float32, -1.0, 1.0) * block_scale(seeds[6], (LAYERS, SHEADS), ((1, 2),), -0.4, 0.0), -1.0, 1.0)
    decay_rate = draw_decay_rate(jax.random.fold_in(seeds[10], 71), 0)
    skip_gain = jnp.clip(0.5 + 1.5 * jax.random.uniform(seeds[8], (LAYERS, SHEADS), jnp.float32) ** block_scale(seeds[8], (LAYERS, SHEADS), ((1, 2),), -0.2, 0.2), 0.5, 2.0)
    out_gain = jnp.clip(1.0 + 0.1 * jax.random.normal(seeds[9], (LAYERS, SHEADS, SHEAD), jnp.float32), 0.5, 1.5)
    return dict(queries=queries, keys=keys, values=values, layer_in=layer_in, w_bc=w_bc, w_dt=w_dt, dt_bias=dt_bias, decay_rate=decay_rate, skip_gain=skip_gain, out_gain=out_gain)


EPSILON = 1e-05

def span_terms(normed, b_rows, c_rows, step_sizes, rate_row, skip_row):
    count_rows, head_count, head_width = normed.shape
    group_count = b_rows.shape[1]
    per_group = head_count // group_count
    state_root = math.sqrt(b_rows.shape[2])
    log_decay = jnp.cumsum(-step_sizes * rate_row[None, :], axis=0)
    lower_mask = jnp.arange(count_rows)[:, None] >= jnp.arange(count_rows)[None, :]
    intersection = jnp.einsum('tgn,sgn->gts', c_rows, b_rows, precision=lax.Precision.HIGHEST) / state_root
    log_gaps = log_decay.T[:, :, None] - log_decay.T[:, None, :]
    decays = jnp.where(lower_mask[None], jnp.exp(jnp.where(lower_mask[None], log_gaps, 0.0)), 0.0)
    mixing = decays.reshape(group_count, per_group, count_rows, count_rows) * intersection[:, None] * step_sizes.T.reshape(group_count, per_group, 1, count_rows)
    grouped = normed.reshape(count_rows, group_count, per_group, head_width)
    local_part = jnp.einsum('gkts,sgkp->tgkp', mixing, grouped, precision=lax.Precision.HIGHEST).reshape(count_rows, head_count, head_width)
    tail_weight = jnp.exp(log_decay[-1][None, :] - log_decay) * step_sizes
    weighted = (normed * tail_weight[:, :, None]).reshape(count_rows, group_count, per_group, head_width)
    ending = jnp.einsum('sgkp,sgn->gkpn', weighted, b_rows, precision=lax.Precision.HIGHEST).reshape(head_count, head_width, b_rows.shape[2])
    return (log_decay, local_part + skip_row[None, :, None] * normed, ending, jnp.exp(log_decay[-1]))

def span_inflow(log_decay, c_rows, state_in):
    count_rows, group_count, state_n = c_rows.shape
    head_count, head_width = (state_in.shape[0], state_in.shape[1])
    per_group = head_count // group_count
    state_root = math.sqrt(state_n)
    inflow = jnp.einsum('tgn,gkpn->tgkp', c_rows, state_in.reshape(group_count, per_group, head_width, state_n), precision=lax.Precision.HIGHEST)
    return jnp.exp(log_decay)[:, :, None] * inflow.reshape(count_rows, head_count, head_width) / state_root

def attend_one(queries, keys, values):
    group_size = queries.shape[1] // keys.shape[1]
    score_scale = 1.0 / math.sqrt(queries.shape[2])
    positions = jnp.arange(queries.shape[0])
    causal = positions[:, None] >= positions[None, :]

    def one_head(head_index):
        q_one = lax.dynamic_index_in_dim(queries, head_index, 1, keepdims=False)
        k_one = lax.dynamic_index_in_dim(keys, head_index // group_size, 1, keepdims=False)
        v_one = lax.dynamic_index_in_dim(values, head_index // group_size, 1, keepdims=False)
        scores = jnp.dot(q_one, k_one.T, preferred_element_type=jnp.float32) * score_scale
        scores = jnp.where(causal, scores, -jnp.inf)
        row_top = lax.optimization_barrier(jnp.max(scores, axis=1, keepdims=True))
        raw_weight = jnp.exp(scores - row_top)
        row_total = lax.optimization_barrier(jnp.sum(raw_weight, axis=1, keepdims=True))
        mixed_out = jnp.dot(raw_weight.astype(jnp.bfloat16), v_one, preferred_element_type=jnp.float32) / row_total
        return mixed_out.astype(jnp.bfloat16)
    heads_out = lax.map(one_head, jnp.arange(queries.shape[1], dtype=jnp.int32))
    return heads_out.transpose(1, 0, 2).reshape(queries.shape[0], queries.shape[1] * queries.shape[2])

def state_layer(inputs, w_bc, w_dt, dt_bias, decay_rate, skip_gain, out_gain):
    seq_len, channel_count = inputs.shape
    head_count = decay_rate.shape[0]
    head_width = channel_count // head_count
    proj_bc = jnp.dot(inputs, w_bc, preferred_element_type=jnp.float32)
    proj_dt = jnp.dot(inputs, w_dt, preferred_element_type=jnp.float32)
    wide_rows = inputs.astype(jnp.float32)
    inv_rms = lax.rsqrt(lax.optimization_barrier(jnp.sum(wide_rows * wide_rows, axis=1)) / channel_count + EPSILON)
    normed = (wide_rows * inv_rms[:, None]).reshape(seq_len, head_count, head_width)
    half_cols = w_bc.shape[1] // 2
    b_rows = (proj_bc[:, :half_cols] * inv_rms[:, None]).reshape(seq_len, GROUPS, STATE)
    c_rows = (proj_bc[:, half_cols:] * inv_rms[:, None]).reshape(seq_len, GROUPS, STATE)
    step_sizes = jax.nn.softplus(proj_dt * inv_rms[:, None] + dt_bias[None, :])
    block_count = seq_len // L_DEV

    def split_rows(array):
        return array.reshape((block_count, L_DEV) + array.shape[1:])

    def one_block(carried, pieces):
        normed_b, b_b, c_b, step_b = pieces
        log_decay, local_part, ending, span_decay = span_terms(normed_b, b_b, c_b, step_b, decay_rate, skip_gain)
        mixed_out = local_part + span_inflow(log_decay, c_b, carried)
        return (span_decay[:, None, None] * carried + ending, mixed_out)
    initial = jnp.zeros((head_count, head_width, STATE), jnp.float32)
    _, mixed_blocks = lax.scan(one_block, initial, (split_rows(normed), split_rows(b_rows), split_rows(c_rows), split_rows(step_sizes)))
    mixed_out = mixed_blocks.reshape(seq_len, head_count, head_width)
    power = lax.optimization_barrier(jnp.mean(mixed_out * mixed_out, axis=2, keepdims=True))
    result = wide_rows.reshape(seq_len, head_count, head_width) + out_gain[None] * mixed_out * lax.rsqrt(power + EPSILON)
    return result.reshape(seq_len, channel_count).astype(jnp.bfloat16)

def reference(queries, keys, values, layer_in, w_bc, w_dt, dt_bias, decay_rate, skip_gain, out_gain):
    attended = attend_one(queries, keys, values)
    current = layer_in
    for layer_index in range(LAYERS):
        current = state_layer(current, w_bc[layer_index], w_dt[layer_index], dt_bias[layer_index], decay_rate[layer_index], skip_gain[layer_index], out_gain[layer_index])
    return jnp.stack([current, attended])
```

```python
import math

import jax
import jax.numpy as jnp
from jax import lax
from jax.sharding import PartitionSpec as P

GROUPS = 4
STATE = 128


EPSILON = 1e-05


def shifted_up(value, axis, distance):
    size = lax.axis_size(axis)
    pairs = [(source, source + distance) for source in range(size - distance)]
    return lax.ppermute(value, axis, pairs)


def swapped(value, axis):
    return lax.ppermute(value, axis, [(0, 1), (1, 0)])


def span_terms(normed, b_rows, c_rows, step_sizes, rate_row, skip_row):
    count_rows, head_count, head_width = normed.shape
    group_count = b_rows.shape[1]
    per_group = head_count // group_count
    state_root = math.sqrt(b_rows.shape[2])
    log_decay = jnp.cumsum(-step_sizes * rate_row[None, :], axis=0)
    lower_mask = jnp.arange(count_rows)[:, None] >= jnp.arange(count_rows)[None, :]
    intersection = (
        jnp.einsum("tgn,sgn->gts", c_rows, b_rows, precision=lax.Precision.HIGHEST) / state_root
    )
    log_gaps = log_decay.T[:, :, None] - log_decay.T[:, None, :]
    decays = jnp.where(lower_mask[None], jnp.exp(jnp.where(lower_mask[None], log_gaps, 0.0)), 0.0)
    mixing = (
        decays.reshape(group_count, per_group, count_rows, count_rows)
        * intersection[:, None]
        * step_sizes.T.reshape(group_count, per_group, 1, count_rows)
    )
    grouped = normed.reshape(count_rows, group_count, per_group, head_width)
    local_part = jnp.einsum(
        "gkts,sgkp->tgkp", mixing, grouped, precision=lax.Precision.HIGHEST
    ).reshape(count_rows, head_count, head_width)
    tail_weight = jnp.exp(log_decay[-1][None, :] - log_decay) * step_sizes
    weighted = (normed * tail_weight[:, :, None]).reshape(
        count_rows, group_count, per_group, head_width
    )
    ending = jnp.einsum(
        "sgkp,sgn->gkpn", weighted, b_rows, precision=lax.Precision.HIGHEST
    ).reshape(head_count, head_width, b_rows.shape[2])
    return (
        log_decay,
        local_part + skip_row[None, :, None] * normed,
        ending,
        jnp.exp(log_decay[-1]),
    )


def span_inflow(log_decay, c_rows, state_in):
    count_rows, group_count, state_n = c_rows.shape
    head_count, head_width = (state_in.shape[0], state_in.shape[1])
    per_group = head_count // group_count
    state_root = math.sqrt(state_n)
    inflow = jnp.einsum(
        "tgn,gkpn->tgkp",
        c_rows,
        state_in.reshape(group_count, per_group, head_width, state_n),
        precision=lax.Precision.HIGHEST,
    )
    return (
        jnp.exp(log_decay)[:, :, None]
        * inflow.reshape(count_rows, head_count, head_width)
        / state_root
    )


def merge_states(earlier, later):
    return (earlier[0] * later[0], later[0][:, None, None] * earlier[1] + later[1])


def exclusive_scan(decay, state, axis):
    place = lax.axis_index(axis)
    size = lax.axis_size(axis)
    incl = (decay, state)
    excl = (jnp.ones_like(decay), jnp.zeros_like(state))
    distance = 1
    while distance < size:
        got = jax.tree.map(lambda a: shifted_up(a, axis, distance), incl)
        present = place >= distance
        got = (jnp.where(present, got[0], 1.0), jnp.where(present, got[1], 0.0))
        excl = merge_states(got, excl)
        if distance * 2 < size:
            incl = merge_states(got, incl)
        distance *= 2
    return excl


def attention_half(queries, keys, values, first_row):
    row_count, q_heads, head_width = queries.shape
    kv_heads = keys.shape[1]
    group_size = q_heads // kv_heads
    score_scale = 1.0 / math.sqrt(head_width)
    last_row = first_row + row_count - 1
    query_place = first_row + jnp.arange(row_count, dtype=jnp.int32)
    grouped = queries.reshape(row_count, kv_heads, group_size, head_width).transpose(1, 2, 0, 3)
    both = jnp.concatenate([keys, values], axis=1)
    both_all = lax.all_gather(both, "ctx", axis=0, tiled=True)
    key_count = both_all.shape[0]
    block_size = math.gcd(key_count, 1024)

    def add_block(block_index, carried):
        row_top, row_total, row_sum = carried
        block_start = block_index * block_size
        block = lax.dynamic_slice_in_dim(both_all, block_start, block_size, 0)
        key_block = block[:, :kv_heads]
        value_block = block[:, kv_heads:]
        scores = (
            jnp.einsum("kgqd,skd->kgqs", grouped, key_block, preferred_element_type=jnp.float32)
            * score_scale
        )
        key_place = block_start + jnp.arange(block_size, dtype=jnp.int32)
        allowed = (query_place[:, None] >= key_place[None, :])[None, None]
        masked = jnp.where(allowed, scores, -1e30)
        new_top = jnp.maximum(row_top, jnp.max(masked, axis=3))
        raw_weight = jnp.where(allowed, jnp.exp(masked - new_top[..., None]), 0.0)
        factor = jnp.exp(row_top - new_top)
        new_total = row_total * factor + jnp.sum(raw_weight, axis=3)
        block_sum = jnp.einsum(
            "kgqs,skd->kgqd",
            raw_weight.astype(jnp.bfloat16),
            value_block,
            preferred_element_type=jnp.float32,
        )
        return (new_top, new_total, row_sum * factor[..., None] + block_sum)

    initial = (
        jnp.full((kv_heads, group_size, row_count), -1e30, jnp.float32),
        jnp.zeros((kv_heads, group_size, row_count), jnp.float32),
        jnp.zeros((kv_heads, group_size, row_count, head_width), jnp.float32),
    )
    block_count = last_row // block_size + 1
    row_top, row_total, row_sum = lax.fori_loop(0, block_count, add_block, initial)
    mixed_out = row_sum / row_total[..., None]
    return (
        mixed_out.transpose(2, 0, 1, 3)
        .reshape(row_count, q_heads * head_width)
        .astype(jnp.bfloat16)
    )


def body(queries, keys, values, layer_in, w_bc, w_dt, dt_bias, decay_rate, skip_gain, out_gain):
    seg = lax.axis_index("segment")
    seg_count = lax.axis_size("segment")
    tp = lax.axis_index("tp")
    tp_count = lax.axis_size("tp")
    row_count, q_heads, head_width = queries.shape
    kv_heads = keys.shape[1]
    first_row = lax.axis_index("ctx") * row_count

    q_share = q_heads // seg_count
    kv_share = kv_heads // seg_count
    q_part = lax.dynamic_slice_in_dim(queries, seg * q_share, q_share, 1)
    k_part = lax.dynamic_slice_in_dim(keys, seg * kv_share, kv_share, 1)
    v_part = lax.dynamic_slice_in_dim(values, seg * kv_share, kv_share, 1)
    attended = attention_half(q_part, k_part, v_part, first_row)

    current = layer_in
    channel_count = current.shape[1]
    heads_dev = dt_bias.shape[1]
    state_width = channel_count // heads_dev
    groups_dev = GROUPS // tp_count
    groups_core = groups_dev // seg_count
    heads_core = heads_dev // seg_count
    half_cols = GROUPS * STATE
    wide_rows = current.astype(jnp.float32)
    part_bc = jnp.dot(current, w_bc[0], preferred_element_type=jnp.float32)
    part_dt = jnp.dot(current, w_dt[0], preferred_element_type=jnp.float32)
    part_sq = jnp.sum(wide_rows * wide_rows, axis=1)

    def columns_for(tp_index):
        group_start = (tp_index * groups_dev + seg * groups_core) * STATE
        head_start = tp_index * heads_dev + seg * heads_core
        return jnp.concatenate(
            [
                lax.dynamic_slice_in_dim(part_bc, group_start, groups_core * STATE, 1),
                lax.dynamic_slice_in_dim(part_bc, half_cols + group_start, groups_core * STATE, 1),
                lax.dynamic_slice_in_dim(part_dt, head_start, heads_core, 1),
                part_sq[:, None],
            ],
            axis=1,
        )

    mine = columns_for(tp)
    theirs = columns_for(tp_count - 1 - tp)
    total = mine + swapped(theirs, "tp")
    width_bc = groups_core * STATE
    sum_b = total[:, :width_bc]
    sum_c = total[:, width_bc : 2 * width_bc]
    sum_dt = total[:, 2 * width_bc : 2 * width_bc + heads_core]
    sum_sq = total[:, 2 * width_bc + heads_core]
    inv_rms = lax.rsqrt(sum_sq / (channel_count * tp_count) + EPSILON)
    own_rows = lax.dynamic_slice_in_dim(wide_rows, seg * heads_core * state_width, heads_core * state_width, 1)
    normed = (own_rows * inv_rms[:, None]).reshape(row_count, heads_core, state_width)
    b_rows = (sum_b * inv_rms[:, None]).reshape(row_count, groups_core, STATE)
    c_rows = (sum_c * inv_rms[:, None]).reshape(row_count, groups_core, STATE)
    bias = lax.dynamic_slice_in_dim(dt_bias[0], seg * heads_core, heads_core, 0)
    rate = lax.dynamic_slice_in_dim(decay_rate[0], seg * heads_core, heads_core, 0)
    skip = lax.dynamic_slice_in_dim(skip_gain[0], seg * heads_core, heads_core, 0)
    gain = lax.dynamic_slice_in_dim(out_gain[0], seg * heads_core, heads_core, 0)
    step_sizes = jax.nn.softplus(sum_dt * inv_rms[:, None] + bias[None, :])

    log_decay, local_part, ending, span_decay = span_terms(
        normed, b_rows, c_rows, step_sizes, rate, skip
    )
    _, state_in = exclusive_scan(span_decay, ending, "ctx")
    mixed_out = local_part + span_inflow(log_decay, c_rows, state_in)
    power = jnp.mean(mixed_out * mixed_out, axis=2, keepdims=True)
    result = own_rows.reshape(row_count, heads_core, state_width) + gain[None] * mixed_out * lax.rsqrt(
        power + EPSILON
    )
    state_part = result.reshape(row_count, heads_core * state_width).astype(jnp.bfloat16)

    keep_state = seg == 0
    outgoing = jnp.where(keep_state, attended, state_part)
    incoming = swapped(outgoing, "segment")
    first = jnp.where(keep_state, state_part, incoming)
    second = jnp.where(keep_state, incoming, attended)
    return jnp.concatenate([first, second], axis=1)[None]


def solution(mesh):
    in_specs = (
        P("ctx", "tp", None),
        P("ctx", "tp", None),
        P("ctx", "tp", None),
        P("ctx", "tp"),
        P(None, "tp", None),
        P(None, "tp", None),
        P(None, "tp"),
        P(None, "tp"),
        P(None, "tp"),
        P(None, "tp", None),
    )
    out_specs = P("segment", "ctx", "tp")
    return jax.shard_map(body, mesh=mesh, in_specs=in_specs, out_specs=out_specs, check_vma=False)
```

```python
import math

import jax
import jax.numpy as jnp
from jax import lax
from jax.sharding import PartitionSpec as P

GROUPS = 4
STATE = 128


EPSILON = 1e-05


def shifted_up(value, axis, distance):
    size = lax.axis_size(axis)
    pairs = [(source, source + distance) for source in range(size - distance)]
    return lax.ppermute(value, axis, pairs)


def swapped(value, axis):
    return lax.ppermute(value, axis, [(0, 1), (1, 0)])


def span_terms(normed, b_rows, c_rows, step_sizes, rate_row, skip_row):
    count_rows, head_count, head_width = normed.shape
    group_count = b_rows.shape[1]
    per_group = head_count // group_count
    state_root = math.sqrt(b_rows.shape[2])
    log_decay = jnp.cumsum(-step_sizes * rate_row[None, :], axis=0)
    lower_mask = jnp.arange(count_rows)[:, None] >= jnp.arange(count_rows)[None, :]
    intersection = (
        jnp.einsum("tgn,sgn->gts", c_rows, b_rows, precision=lax.Precision.HIGHEST) / state_root
    )
    log_gaps = log_decay.T[:, :, None] - log_decay.T[:, None, :]
    decays = jnp.where(lower_mask[None], jnp.exp(jnp.where(lower_mask[None], log_gaps, 0.0)), 0.0)
    mixing = (
        decays.reshape(group_count, per_group, count_rows, count_rows)
        * intersection[:, None]
        * step_sizes.T.reshape(group_count, per_group, 1, count_rows)
    )
    grouped = normed.reshape(count_rows, group_count, per_group, head_width)
    local_part = jnp.einsum(
        "gkts,sgkp->tgkp", mixing, grouped, precision=lax.Precision.HIGHEST
    ).reshape(count_rows, head_count, head_width)
    tail_weight = jnp.exp(log_decay[-1][None, :] - log_decay) * step_sizes
    weighted = (normed * tail_weight[:, :, None]).reshape(
        count_rows, group_count, per_group, head_width
    )
    ending = jnp.einsum(
        "sgkp,sgn->gkpn", weighted, b_rows, precision=lax.Precision.HIGHEST
    ).reshape(head_count, head_width, b_rows.shape[2])
    return (
        log_decay,
        local_part + skip_row[None, :, None] * normed,
        ending,
        jnp.exp(log_decay[-1]),
    )


def span_inflow(log_decay, c_rows, state_in):
    count_rows, group_count, state_n = c_rows.shape
    head_count, head_width = (state_in.shape[0], state_in.shape[1])
    per_group = head_count // group_count
    state_root = math.sqrt(state_n)
    inflow = jnp.einsum(
        "tgn,gkpn->tgkp",
        c_rows,
        state_in.reshape(group_count, per_group, head_width, state_n),
        precision=lax.Precision.HIGHEST,
    )
    return (
        jnp.exp(log_decay)[:, :, None]
        * inflow.reshape(count_rows, head_count, head_width)
        / state_root
    )


def merge_states(earlier, later):
    return (earlier[0] * later[0], later[0][:, None, None] * earlier[1] + later[1])


def exclusive_scan(decay, state, axis, radix=4):
    place = lax.axis_index(axis)
    size = lax.axis_size(axis)
    incl = (decay, state)
    excl = (jnp.ones_like(decay), jnp.zeros_like(state))
    stride = 1
    while stride < size:
        joined = None
        for step in range(radix - 1, 0, -1):
            distance = step * stride
            if distance >= size:
                continue
            got = jax.tree.map(lambda a: shifted_up(a, axis, distance), incl)
            present = place >= distance
            got = (jnp.where(present, got[0], 1.0), jnp.where(present, got[1], 0.0))
            joined = got if joined is None else merge_states(joined, got)
        excl = merge_states(joined, excl)
        if stride * radix < size:
            incl = merge_states(joined, incl)
        stride *= radix
    return excl


def attention_half(queries, keys, values, first_row, radix=4):
    row_count, q_heads, head_width = queries.shape
    kv_heads = keys.shape[1]
    group_size = q_heads // kv_heads
    score_scale = 1.0 / math.sqrt(head_width)
    query_place = first_row + jnp.arange(row_count, dtype=jnp.int32)
    grouped = queries.reshape(row_count, kv_heads, group_size, head_width).transpose(1, 2, 0, 3)
    place = lax.axis_index("ctx")
    size = lax.axis_size("ctx")

    def add_block(carried, block, block_start):
        row_top, row_total, row_sum = carried
        key_block = block[:, :kv_heads]
        value_block = block[:, kv_heads:]
        scores = (
            jnp.einsum("kgqd,skd->kgqs", grouped, key_block, preferred_element_type=jnp.float32)
            * score_scale
        )
        key_place = block_start + jnp.arange(block.shape[0], dtype=jnp.int32)
        allowed = jnp.logical_and(
            query_place[:, None] >= key_place[None, :], key_place[None, :] >= 0
        )[None, None]
        masked = jnp.where(allowed, scores, -1e30)
        new_top = jnp.maximum(row_top, jnp.max(masked, axis=3))
        raw_weight = jnp.where(allowed, jnp.exp(masked - new_top[..., None]), 0.0)
        factor = jnp.exp(row_top - new_top)
        new_total = row_total * factor + jnp.sum(raw_weight, axis=3)
        block_sum = jnp.einsum(
            "kgqs,skd->kgqd",
            raw_weight.astype(jnp.bfloat16),
            value_block,
            preferred_element_type=jnp.float32,
        )
        return (new_top, new_total, row_sum * factor[..., None] + block_sum)

    carried = (
        jnp.full((kv_heads, group_size, row_count), -1e30, jnp.float32),
        jnp.zeros((kv_heads, group_size, row_count), jnp.float32),
        jnp.zeros((kv_heads, group_size, row_count, head_width), jnp.float32),
    )
    held = jnp.concatenate([keys, values], axis=1)
    carried = add_block(carried, held, first_row)
    stride = 1
    while stride < size:
        pieces = []
        for step in range(radix - 1, 0, -1):
            distance = step * stride
            if distance >= size:
                continue
            piece = shifted_up(held, "ctx", distance)
            piece_start = (place - distance - stride + 1) * row_count
            pieces.append(piece)
            carried = add_block(carried, piece, piece_start)
        if stride * radix < size:
            held = jnp.concatenate(pieces + [held], axis=0)
        stride *= radix
    row_top, row_total, row_sum = carried
    mixed_out = row_sum / row_total[..., None]
    return (
        mixed_out.transpose(2, 0, 1, 3)
        .reshape(row_count, q_heads * head_width)
        .astype(jnp.bfloat16)
    )


def body(queries, keys, values, layer_in, w_bc, w_dt, dt_bias, decay_rate, skip_gain, out_gain):
    seg = lax.axis_index("segment")
    seg_count = lax.axis_size("segment")
    tp = lax.axis_index("tp")
    tp_count = lax.axis_size("tp")
    row_count, q_heads, head_width = queries.shape
    kv_heads = keys.shape[1]
    first_row = lax.axis_index("ctx") * row_count

    q_share = q_heads // seg_count
    kv_share = kv_heads // seg_count
    q_part = lax.dynamic_slice_in_dim(queries, seg * q_share, q_share, 1)
    k_part = lax.dynamic_slice_in_dim(keys, seg * kv_share, kv_share, 1)
    v_part = lax.dynamic_slice_in_dim(values, seg * kv_share, kv_share, 1)
    attended = attention_half(q_part, k_part, v_part, first_row)

    current = layer_in
    channel_count = current.shape[1]
    heads_dev = dt_bias.shape[1]
    state_width = channel_count // heads_dev
    groups_dev = GROUPS // tp_count
    groups_core = groups_dev // seg_count
    heads_core = heads_dev // seg_count
    half_cols = GROUPS * STATE
    wide_rows = current.astype(jnp.float32)
    part_bc = jnp.dot(current, w_bc[0], preferred_element_type=jnp.float32)
    part_dt = jnp.dot(current, w_dt[0], preferred_element_type=jnp.float32)
    part_sq = jnp.sum(wide_rows * wide_rows, axis=1)

    def columns_for(tp_index):
        group_start = (tp_index * groups_dev + seg * groups_core) * STATE
        head_start = tp_index * heads_dev + seg * heads_core
        return jnp.concatenate(
            [
                lax.dynamic_slice_in_dim(part_bc, group_start, groups_core * STATE, 1),
                lax.dynamic_slice_in_dim(part_bc, half_cols + group_start, groups_core * STATE, 1),
                lax.dynamic_slice_in_dim(part_dt, head_start, heads_core, 1),
                part_sq[:, None],
            ],
            axis=1,
        )

    mine = columns_for(tp)
    theirs = columns_for(tp_count - 1 - tp)
    total = mine + swapped(theirs, "tp")
    width_bc = groups_core * STATE
    sum_b = total[:, :width_bc]
    sum_c = total[:, width_bc : 2 * width_bc]
    sum_dt = total[:, 2 * width_bc : 2 * width_bc + heads_core]
    sum_sq = total[:, 2 * width_bc + heads_core]
    inv_rms = lax.rsqrt(sum_sq / (channel_count * tp_count) + EPSILON)
    own_rows = lax.dynamic_slice_in_dim(wide_rows, seg * heads_core * state_width, heads_core * state_width, 1)
    normed = (own_rows * inv_rms[:, None]).reshape(row_count, heads_core, state_width)
    b_rows = (sum_b * inv_rms[:, None]).reshape(row_count, groups_core, STATE)
    c_rows = (sum_c * inv_rms[:, None]).reshape(row_count, groups_core, STATE)
    bias = lax.dynamic_slice_in_dim(dt_bias[0], seg * heads_core, heads_core, 0)
    rate = lax.dynamic_slice_in_dim(decay_rate[0], seg * heads_core, heads_core, 0)
    skip = lax.dynamic_slice_in_dim(skip_gain[0], seg * heads_core, heads_core, 0)
    gain = lax.dynamic_slice_in_dim(out_gain[0], seg * heads_core, heads_core, 0)
    step_sizes = jax.nn.softplus(sum_dt * inv_rms[:, None] + bias[None, :])

    log_decay, local_part, ending, span_decay = span_terms(
        normed, b_rows, c_rows, step_sizes, rate, skip
    )
    _, state_in = exclusive_scan(span_decay, ending, "ctx")
    mixed_out = local_part + span_inflow(log_decay, c_rows, state_in)
    power = jnp.mean(mixed_out * mixed_out, axis=2, keepdims=True)
    result = own_rows.reshape(row_count, heads_core, state_width) + gain[None] * mixed_out * lax.rsqrt(
        power + EPSILON
    )
    state_part = result.reshape(row_count, heads_core * state_width).astype(jnp.bfloat16)

    keep_state = seg == 0
    outgoing = jnp.where(keep_state, attended, state_part)
    incoming = swapped(outgoing, "segment")
    first = jnp.where(keep_state, state_part, incoming)
    second = jnp.where(keep_state, incoming, attended)
    return jnp.concatenate([first, second], axis=1)[None]


def solution(mesh):
    in_specs = (
        P("ctx", "tp", None),
        P("ctx", "tp", None),
        P("ctx", "tp", None),
        P("ctx", "tp"),
        P(None, "tp", None),
        P(None, "tp", None),
        P(None, "tp"),
        P(None, "tp"),
        P(None, "tp"),
        P(None, "tp", None),
    )
    out_specs = P("segment", "ctx", "tp")
    return jax.shard_map(body, mesh=mesh, in_specs=in_specs, out_specs=out_specs, check_vma=False)
```

```python
import functools
import math

import jax
import jax.numpy as jnp
from jax import lax
from jax.experimental import pallas as pl
from jax.experimental.pallas import tpu as pltpu
from jax.sharding import PartitionSpec as P

GROUPS = 4
STATE = 128


EPSILON = 1e-05


def shifted_up(value, axis, distance):
    size = lax.axis_size(axis)
    pairs = [(source, source + distance) for source in range(size - distance)]
    return lax.ppermute(value, axis, pairs)


def swapped(value, axis):
    return lax.ppermute(value, axis, [(0, 1), (1, 0)])


def span_terms(normed, b_rows, c_rows, step_sizes, rate_row, skip_row):
    count_rows, head_count, head_width = normed.shape
    group_count = b_rows.shape[1]
    per_group = head_count // group_count
    state_root = math.sqrt(b_rows.shape[2])
    log_decay = jnp.cumsum(-step_sizes * rate_row[None, :], axis=0)
    lower_mask = jnp.arange(count_rows)[:, None] >= jnp.arange(count_rows)[None, :]
    intersection = (
        jnp.einsum("tgn,sgn->gts", c_rows, b_rows, precision=lax.Precision.HIGHEST) / state_root
    )
    log_gaps = log_decay.T[:, :, None] - log_decay.T[:, None, :]
    decays = jnp.where(lower_mask[None], jnp.exp(jnp.where(lower_mask[None], log_gaps, 0.0)), 0.0)
    mixing = (
        decays.reshape(group_count, per_group, count_rows, count_rows)
        * intersection[:, None]
        * step_sizes.T.reshape(group_count, per_group, 1, count_rows)
    )
    grouped = normed.reshape(count_rows, group_count, per_group, head_width)
    local_part = jnp.einsum(
        "gkts,sgkp->tgkp", mixing, grouped, precision=lax.Precision.HIGHEST
    ).reshape(count_rows, head_count, head_width)
    tail_weight = jnp.exp(log_decay[-1][None, :] - log_decay) * step_sizes
    weighted = (normed * tail_weight[:, :, None]).reshape(
        count_rows, group_count, per_group, head_width
    )
    ending = jnp.einsum(
        "sgkp,sgn->gkpn", weighted, b_rows, precision=lax.Precision.HIGHEST
    ).reshape(head_count, head_width, b_rows.shape[2])
    return (
        log_decay,
        local_part + skip_row[None, :, None] * normed,
        ending,
        jnp.exp(log_decay[-1]),
    )


def span_inflow(log_decay, c_rows, state_in):
    count_rows, group_count, state_n = c_rows.shape
    head_count, head_width = (state_in.shape[0], state_in.shape[1])
    per_group = head_count // group_count
    state_root = math.sqrt(state_n)
    inflow = jnp.einsum(
        "tgn,gkpn->tgkp",
        c_rows,
        state_in.reshape(group_count, per_group, head_width, state_n),
        precision=lax.Precision.HIGHEST,
    )
    return (
        jnp.exp(log_decay)[:, :, None]
        * inflow.reshape(count_rows, head_count, head_width)
        / state_root
    )


def merge_states(earlier, later):
    return (earlier[0] * later[0], later[0][:, None, None] * earlier[1] + later[1])


def exclusive_scan(decay, state, axis, radix=4):
    place = lax.axis_index(axis)
    size = lax.axis_size(axis)
    incl = (decay, state)
    excl = (jnp.ones_like(decay), jnp.zeros_like(state))
    stride = 1
    while stride < size:
        joined = None
        for step in range(radix - 1, 0, -1):
            distance = step * stride
            if distance >= size:
                continue
            got = jax.tree.map(lambda a: shifted_up(a, axis, distance), incl)
            present = place >= distance
            got = (jnp.where(present, got[0], 1.0), jnp.where(present, got[1], 0.0))
            joined = got if joined is None else merge_states(joined, got)
        excl = merge_states(joined, excl)
        if stride * radix < size:
            incl = merge_states(joined, incl)
        stride *= radix
    return excl


def flash_kernel(first_ref, q_ref, k_ref, v_ref, o_ref, top_ref, total_ref, acc_ref, *, row_count, key_block, scale):
    j = pl.program_id(1)

    @pl.when(j == 0)
    def _():
        top_ref[...] = jnp.full(top_ref.shape, -1e30, jnp.float32)
        total_ref[...] = jnp.zeros(total_ref.shape, jnp.float32)
        acc_ref[...] = jnp.zeros(acc_ref.shape, jnp.float32)

    first = first_ref[0]

    @pl.when(j * key_block <= first + row_count - 1)
    def _():
        scores = (
            lax.dot_general(
                q_ref[...], k_ref[...], (((1,), (1,)), ((), ())), preferred_element_type=jnp.float32
            )
            * scale
        )
        rows = lax.broadcasted_iota(jnp.int32, scores.shape, 0) % row_count + first
        cols = lax.broadcasted_iota(jnp.int32, scores.shape, 1) + j * key_block
        allowed = rows >= cols
        masked = jnp.where(allowed, scores, -1e30)
        row_top = top_ref[...]
        new_top = jnp.maximum(row_top, jnp.max(masked, axis=1, keepdims=True))
        raw_weight = jnp.where(allowed, jnp.exp(masked - new_top), 0.0)
        factor = jnp.exp(row_top - new_top)
        total_ref[...] = total_ref[...] * factor + jnp.sum(raw_weight, axis=1, keepdims=True)
        acc_ref[...] = acc_ref[...] * factor + jnp.dot(
            raw_weight.astype(jnp.bfloat16), v_ref[...], preferred_element_type=jnp.float32
        )
        top_ref[...] = new_top

    @pl.when(j == pl.num_programs(1) - 1)
    def _():
        o_ref[...] = (acc_ref[...] / total_ref[...]).astype(o_ref.dtype)


def attention_half(queries, keys, values, first_row):
    row_count, q_heads, head_width = queries.shape
    kv_heads = keys.shape[1]
    group_size = q_heads // kv_heads
    score_scale = 1.0 / math.sqrt(head_width)
    grouped = (
        queries.reshape(row_count, kv_heads, group_size, head_width)
        .transpose(1, 2, 0, 3)
        .reshape(kv_heads, group_size * row_count, head_width)
    )
    both = jnp.concatenate([keys, values], axis=1).transpose(1, 0, 2)
    both_all = lax.all_gather(both, "ctx", axis=1, tiled=True)
    key_count = both_all.shape[1]
    key_block = math.gcd(key_count, 512)
    rows = group_size * row_count

    def key_index(h, j, first_ref):
        return (h, jnp.minimum(j, (first_ref[0] + row_count - 1) // key_block), 0)

    def value_index(h, j, first_ref):
        return (kv_heads + h, jnp.minimum(j, (first_ref[0] + row_count - 1) // key_block), 0)

    out = pl.pallas_call(
        functools.partial(flash_kernel, row_count=row_count, key_block=key_block, scale=score_scale),
        out_shape=jax.ShapeDtypeStruct((kv_heads, rows, head_width), jnp.bfloat16),
        grid_spec=pltpu.PrefetchScalarGridSpec(
            num_scalar_prefetch=1,
            grid=(kv_heads, key_count // key_block),
            in_specs=[
                pl.BlockSpec((None, rows, head_width), lambda h, j, f: (h, 0, 0)),
                pl.BlockSpec((None, key_block, head_width), key_index),
                pl.BlockSpec((None, key_block, head_width), value_index),
            ],
            out_specs=pl.BlockSpec((None, rows, head_width), lambda h, j, f: (h, 0, 0)),
            scratch_shapes=[
                pltpu.VMEM((rows, 1), jnp.float32),
                pltpu.VMEM((rows, 1), jnp.float32),
                pltpu.VMEM((rows, head_width), jnp.float32),
            ],
        ),
        compiler_params=pltpu.CompilerParams(dimension_semantics=("parallel", "arbitrary")),
    )(jnp.reshape(first_row, (1,)).astype(jnp.int32), grouped, both_all, both_all)
    return (
        out.reshape(kv_heads, group_size, row_count, head_width)
        .transpose(2, 0, 1, 3)
        .reshape(row_count, q_heads * head_width)
    )


def body(queries, keys, values, layer_in, w_bc, w_dt, dt_bias, decay_rate, skip_gain, out_gain):
    seg = lax.axis_index("segment")
    seg_count = lax.axis_size("segment")
    tp = lax.axis_index("tp")
    tp_count = lax.axis_size("tp")
    row_count, q_heads, head_width = queries.shape
    kv_heads = keys.shape[1]
    first_row = lax.axis_index("ctx") * row_count

    q_share = q_heads // seg_count
    kv_share = kv_heads // seg_count
    q_part = lax.dynamic_slice_in_dim(queries, seg * q_share, q_share, 1)
    k_part = lax.dynamic_slice_in_dim(keys, seg * kv_share, kv_share, 1)
    v_part = lax.dynamic_slice_in_dim(values, seg * kv_share, kv_share, 1)
    attended = attention_half(q_part, k_part, v_part, first_row)

    current = layer_in
    channel_count = current.shape[1]
    heads_dev = dt_bias.shape[1]
    state_width = channel_count // heads_dev
    groups_dev = GROUPS // tp_count
    groups_core = groups_dev // seg_count
    heads_core = heads_dev // seg_count
    half_cols = GROUPS * STATE
    wide_rows = current.astype(jnp.float32)
    part_bc = jnp.dot(current, w_bc[0], preferred_element_type=jnp.float32)
    part_dt = jnp.dot(current, w_dt[0], preferred_element_type=jnp.float32)
    part_sq = jnp.sum(wide_rows * wide_rows, axis=1)

    def columns_for(tp_index):
        group_start = (tp_index * groups_dev + seg * groups_core) * STATE
        head_start = tp_index * heads_dev + seg * heads_core
        return jnp.concatenate(
            [
                lax.dynamic_slice_in_dim(part_bc, group_start, groups_core * STATE, 1),
                lax.dynamic_slice_in_dim(part_bc, half_cols + group_start, groups_core * STATE, 1),
                lax.dynamic_slice_in_dim(part_dt, head_start, heads_core, 1),
                part_sq[:, None],
            ],
            axis=1,
        )

    mine = columns_for(tp)
    theirs = columns_for(tp_count - 1 - tp)
    total = mine + swapped(theirs, "tp")
    width_bc = groups_core * STATE
    sum_b = total[:, :width_bc]
    sum_c = total[:, width_bc : 2 * width_bc]
    sum_dt = total[:, 2 * width_bc : 2 * width_bc + heads_core]
    sum_sq = total[:, 2 * width_bc + heads_core]
    inv_rms = lax.rsqrt(sum_sq / (channel_count * tp_count) + EPSILON)
    own_rows = lax.dynamic_slice_in_dim(wide_rows, seg * heads_core * state_width, heads_core * state_width, 1)
    normed = (own_rows * inv_rms[:, None]).reshape(row_count, heads_core, state_width)
    b_rows = (sum_b * inv_rms[:, None]).reshape(row_count, groups_core, STATE)
    c_rows = (sum_c * inv_rms[:, None]).reshape(row_count, groups_core, STATE)
    bias = lax.dynamic_slice_in_dim(dt_bias[0], seg * heads_core, heads_core, 0)
    rate = lax.dynamic_slice_in_dim(decay_rate[0], seg * heads_core, heads_core, 0)
    skip = lax.dynamic_slice_in_dim(skip_gain[0], seg * heads_core, heads_core, 0)
    gain = lax.dynamic_slice_in_dim(out_gain[0], seg * heads_core, heads_core, 0)
    step_sizes = jax.nn.softplus(sum_dt * inv_rms[:, None] + bias[None, :])

    log_decay, local_part, ending, span_decay = span_terms(
        normed, b_rows, c_rows, step_sizes, rate, skip
    )
    _, state_in = exclusive_scan(span_decay, ending, "ctx")
    mixed_out = local_part + span_inflow(log_decay, c_rows, state_in)
    power = jnp.mean(mixed_out * mixed_out, axis=2, keepdims=True)
    result = own_rows.reshape(row_count, heads_core, state_width) + gain[None] * mixed_out * lax.rsqrt(
        power + EPSILON
    )
    state_part = result.reshape(row_count, heads_core * state_width).astype(jnp.bfloat16)

    keep_state = seg == 0
    outgoing = jnp.where(keep_state, attended, state_part)
    incoming = swapped(outgoing, "segment")
    first = jnp.where(keep_state, state_part, incoming)
    second = jnp.where(keep_state, incoming, attended)
    return jnp.concatenate([first, second], axis=1)[None]


def solution(mesh):
    in_specs = (
        P("ctx", "tp", None),
        P("ctx", "tp", None),
        P("ctx", "tp", None),
        P("ctx", "tp"),
        P(None, "tp", None),
        P(None, "tp", None),
        P(None, "tp"),
        P(None, "tp"),
        P(None, "tp"),
        P(None, "tp", None),
    )
    out_specs = P("segment", "ctx", "tp")
    return jax.shard_map(body, mesh=mesh, in_specs=in_specs, out_specs=out_specs, check_vma=False)
```

```python
import functools
import math

import jax
import jax.numpy as jnp
from jax import lax
from jax.experimental import pallas as pl
from jax.experimental.pallas import tpu as pltpu
from jax.sharding import PartitionSpec as P

GROUPS = 4
STATE = 128


EPSILON = 1e-05


def shifted_up(value, axis, distance):
    size = lax.axis_size(axis)
    pairs = [(source, source + distance) for source in range(size - distance)]
    return lax.ppermute(value, axis, pairs)


def swapped(value, axis):
    return lax.ppermute(value, axis, [(0, 1), (1, 0)])


def span_terms(normed, b_rows, c_rows, step_sizes, rate_row, skip_row):
    count_rows, head_count, head_width = normed.shape
    group_count = b_rows.shape[1]
    per_group = head_count // group_count
    state_root = math.sqrt(b_rows.shape[2])
    log_decay = jnp.cumsum(-step_sizes * rate_row[None, :], axis=0)
    lower_mask = jnp.arange(count_rows)[:, None] >= jnp.arange(count_rows)[None, :]
    intersection = (
        jnp.einsum("tgn,sgn->gts", c_rows, b_rows, precision=lax.Precision.HIGHEST) / state_root
    )
    log_gaps = log_decay.T[:, :, None] - log_decay.T[:, None, :]
    decays = jnp.where(lower_mask[None], jnp.exp(jnp.where(lower_mask[None], log_gaps, 0.0)), 0.0)
    mixing = (
        decays.reshape(group_count, per_group, count_rows, count_rows)
        * intersection[:, None]
        * step_sizes.T.reshape(group_count, per_group, 1, count_rows)
    )
    grouped = normed.reshape(count_rows, group_count, per_group, head_width)
    local_part = jnp.einsum(
        "gkts,sgkp->tgkp", mixing, grouped, precision=lax.Precision.HIGHEST
    ).reshape(count_rows, head_count, head_width)
    tail_weight = jnp.exp(log_decay[-1][None, :] - log_decay) * step_sizes
    weighted = (normed * tail_weight[:, :, None]).reshape(
        count_rows, group_count, per_group, head_width
    )
    ending = jnp.einsum(
        "sgkp,sgn->gkpn", weighted, b_rows, precision=lax.Precision.HIGHEST
    ).reshape(head_count, head_width, b_rows.shape[2])
    return (
        log_decay,
        local_part + skip_row[None, :, None] * normed,
        ending,
        jnp.exp(log_decay[-1]),
    )


def span_inflow(log_decay, c_rows, state_in):
    count_rows, group_count, state_n = c_rows.shape
    head_count, head_width = (state_in.shape[0], state_in.shape[1])
    per_group = head_count // group_count
    state_root = math.sqrt(state_n)
    inflow = jnp.einsum(
        "tgn,gkpn->tgkp",
        c_rows,
        state_in.reshape(group_count, per_group, head_width, state_n),
        precision=lax.Precision.HIGHEST,
    )
    return (
        jnp.exp(log_decay)[:, :, None]
        * inflow.reshape(count_rows, head_count, head_width)
        / state_root
    )


def merge_states(earlier, later):
    return (earlier[0] * later[0], later[0][:, None, None] * earlier[1] + later[1])


def exclusive_scan(decay, state, axis, radix=2):
    place = lax.axis_index(axis)
    size = lax.axis_size(axis)
    incl = (decay, state)
    excl = (jnp.ones_like(decay), jnp.zeros_like(state))
    stride = 1
    while stride < size:
        joined = None
        for step in range(radix - 1, 0, -1):
            distance = step * stride
            if distance >= size:
                continue
            got = jax.tree.map(lambda a: shifted_up(a, axis, distance), incl)
            present = place >= distance
            got = (jnp.where(present, got[0], 1.0), jnp.where(present, got[1], 0.0))
            joined = got if joined is None else merge_states(joined, got)
        excl = merge_states(joined, excl)
        if stride * radix < size:
            incl = merge_states(joined, incl)
        stride *= radix
    return excl


def flash_kernel(first_ref, q_ref, k_ref, v_ref, o_ref, top_ref, total_ref, acc_ref, *, row_count, key_block, scale):
    j = pl.program_id(1)
    first = first_ref[0]
    block_start = j * key_block

    @pl.when(j == 0)
    def _():
        top_ref[...] = jnp.full(top_ref.shape, -1e30, jnp.float32)
        total_ref[...] = jnp.zeros(total_ref.shape, jnp.float32)
        acc_ref[...] = jnp.zeros(acc_ref.shape, jnp.float32)

    def update(with_mask):
        scores = (
            lax.dot_general(
                q_ref[...], k_ref[...], (((1,), (1,)), ((), ())), preferred_element_type=jnp.float32
            )
            * scale
        )
        if with_mask:
            rows = lax.broadcasted_iota(jnp.int32, (scores.shape[0], 1), 0) % row_count + first
            cols = lax.broadcasted_iota(jnp.int32, (1, scores.shape[1]), 1) + block_start
            allowed = rows >= cols
            scores = jnp.where(allowed, scores, -1e30)
        row_top = top_ref[...]
        new_top = jnp.maximum(row_top, jnp.max(scores, axis=1, keepdims=True))
        raw_weight = jnp.exp(scores - new_top)
        if with_mask:
            raw_weight = jnp.where(allowed, raw_weight, 0.0)
        factor = jnp.exp(row_top - new_top)
        total_ref[...] = total_ref[...] * factor + jnp.sum(raw_weight, axis=1, keepdims=True)
        acc_ref[...] = acc_ref[...] * factor + jnp.dot(
            raw_weight.astype(jnp.bfloat16), v_ref[...], preferred_element_type=jnp.float32
        )
        top_ref[...] = new_top

    @pl.when(block_start + key_block - 1 <= first)
    def _():
        update(False)

    @pl.when(
        jnp.logical_and(block_start + key_block - 1 > first, block_start <= first + row_count - 1)
    )
    def _():
        update(True)

    @pl.when(j == pl.num_programs(1) - 1)
    def _():
        o_ref[...] = (acc_ref[...] / total_ref[...]).astype(o_ref.dtype)


def attention_half(queries, keys, values, first_row):
    row_count, q_heads, head_width = queries.shape
    kv_heads = keys.shape[1]
    group_size = q_heads // kv_heads
    score_scale = 1.0 / math.sqrt(head_width)
    grouped = (
        queries.reshape(row_count, kv_heads, group_size, head_width)
        .transpose(1, 2, 0, 3)
        .reshape(kv_heads, group_size * row_count, head_width)
    )
    both = jnp.concatenate([keys, values], axis=1).transpose(1, 0, 2)
    both_all = lax.all_gather(both, "ctx", axis=1, tiled=True)
    key_count = both_all.shape[1]
    key_block = math.gcd(key_count, 1024)
    rows = group_size * row_count

    def key_index(h, j, first_ref):
        return (h, jnp.minimum(j, (first_ref[0] + row_count - 1) // key_block), 0)

    def value_index(h, j, first_ref):
        return (kv_heads + h, jnp.minimum(j, (first_ref[0] + row_count - 1) // key_block), 0)

    out = pl.pallas_call(
        functools.partial(flash_kernel, row_count=row_count, key_block=key_block, scale=score_scale),
        out_shape=jax.ShapeDtypeStruct((kv_heads, rows, head_width), jnp.bfloat16),
        grid_spec=pltpu.PrefetchScalarGridSpec(
            num_scalar_prefetch=1,
            grid=(kv_heads, key_count // key_block),
            in_specs=[
                pl.BlockSpec((None, rows, head_width), lambda h, j, f: (h, 0, 0)),
                pl.BlockSpec((None, key_block, head_width), key_index),
                pl.BlockSpec((None, key_block, head_width), value_index),
            ],
            out_specs=pl.BlockSpec((None, rows, head_width), lambda h, j, f: (h, 0, 0)),
            scratch_shapes=[
                pltpu.VMEM((rows, 1), jnp.float32),
                pltpu.VMEM((rows, 1), jnp.float32),
                pltpu.VMEM((rows, head_width), jnp.float32),
            ],
        ),
        compiler_params=pltpu.CompilerParams(dimension_semantics=("parallel", "arbitrary")),
    )(jnp.reshape(first_row, (1,)).astype(jnp.int32), grouped, both_all, both_all)
    return (
        out.reshape(kv_heads, group_size, row_count, head_width)
        .transpose(2, 0, 1, 3)
        .reshape(row_count, q_heads * head_width)
    )


def body(queries, keys, values, layer_in, w_bc, w_dt, dt_bias, decay_rate, skip_gain, out_gain):
    seg = lax.axis_index("segment")
    seg_count = lax.axis_size("segment")
    tp = lax.axis_index("tp")
    tp_count = lax.axis_size("tp")
    row_count, q_heads, head_width = queries.shape
    kv_heads = keys.shape[1]
    first_row = lax.axis_index("ctx") * row_count

    q_share = q_heads // seg_count
    kv_share = kv_heads // seg_count
    q_part = lax.dynamic_slice_in_dim(queries, seg * q_share, q_share, 1)
    k_part = lax.dynamic_slice_in_dim(keys, seg * kv_share, kv_share, 1)
    v_part = lax.dynamic_slice_in_dim(values, seg * kv_share, kv_share, 1)
    attended = attention_half(q_part, k_part, v_part, first_row)

    current = layer_in
    channel_count = current.shape[1]
    heads_dev = dt_bias.shape[1]
    state_width = channel_count // heads_dev
    groups_dev = GROUPS // tp_count
    groups_core = groups_dev // seg_count
    heads_core = heads_dev // seg_count
    half_cols = GROUPS * STATE
    wide_rows = current.astype(jnp.float32)
    part_bc = jnp.dot(current, w_bc[0], preferred_element_type=jnp.float32)
    part_dt = jnp.dot(current, w_dt[0], preferred_element_type=jnp.float32)
    part_sq = jnp.sum(wide_rows * wide_rows, axis=1)

    def columns_for(tp_index):
        group_start = (tp_index * groups_dev + seg * groups_core) * STATE
        head_start = tp_index * heads_dev + seg * heads_core
        return jnp.concatenate(
            [
                lax.dynamic_slice_in_dim(part_bc, group_start, groups_core * STATE, 1),
                lax.dynamic_slice_in_dim(part_bc, half_cols + group_start, groups_core * STATE, 1),
                lax.dynamic_slice_in_dim(part_dt, head_start, heads_core, 1),
                part_sq[:, None],
            ],
            axis=1,
        )

    mine = columns_for(tp)
    theirs = columns_for(tp_count - 1 - tp)
    total = mine + swapped(theirs, "tp")
    width_bc = groups_core * STATE
    sum_b = total[:, :width_bc]
    sum_c = total[:, width_bc : 2 * width_bc]
    sum_dt = total[:, 2 * width_bc : 2 * width_bc + heads_core]
    sum_sq = total[:, 2 * width_bc + heads_core]
    inv_rms = lax.rsqrt(sum_sq / (channel_count * tp_count) + EPSILON)
    own_rows = lax.dynamic_slice_in_dim(wide_rows, seg * heads_core * state_width, heads_core * state_width, 1)
    normed = (own_rows * inv_rms[:, None]).reshape(row_count, heads_core, state_width)
    b_rows = (sum_b * inv_rms[:, None]).reshape(row_count, groups_core, STATE)
    c_rows = (sum_c * inv_rms[:, None]).reshape(row_count, groups_core, STATE)
    bias = lax.dynamic_slice_in_dim(dt_bias[0], seg * heads_core, heads_core, 0)
    rate = lax.dynamic_slice_in_dim(decay_rate[0], seg * heads_core, heads_core, 0)
    skip = lax.dynamic_slice_in_dim(skip_gain[0], seg * heads_core, heads_core, 0)
    gain = lax.dynamic_slice_in_dim(out_gain[0], seg * heads_core, heads_core, 0)
    step_sizes = jax.nn.softplus(sum_dt * inv_rms[:, None] + bias[None, :])

    log_decay, local_part, ending, span_decay = span_terms(
        normed, b_rows, c_rows, step_sizes, rate, skip
    )
    _, state_in = exclusive_scan(span_decay, ending, "ctx")
    mixed_out = local_part + span_inflow(log_decay, c_rows, state_in)
    power = jnp.mean(mixed_out * mixed_out, axis=2, keepdims=True)
    result = own_rows.reshape(row_count, heads_core, state_width) + gain[None] * mixed_out * lax.rsqrt(
        power + EPSILON
    )
    state_part = result.reshape(row_count, heads_core * state_width).astype(jnp.bfloat16)

    keep_state = seg == 0
    outgoing = jnp.where(keep_state, attended, state_part)
    incoming = swapped(outgoing, "segment")
    first = jnp.where(keep_state, state_part, incoming)
    second = jnp.where(keep_state, incoming, attended)
    return jnp.concatenate([first, second], axis=1)[None]


def solution(mesh):
    in_specs = (
        P("ctx", "tp", None),
        P("ctx", "tp", None),
        P("ctx", "tp", None),
        P("ctx", "tp"),
        P(None, "tp", None),
        P(None, "tp", None),
        P(None, "tp"),
        P(None, "tp"),
        P(None, "tp"),
        P(None, "tp", None),
    )
    out_specs = P("segment", "ctx", "tp")
    return jax.shard_map(body, mesh=mesh, in_specs=in_specs, out_specs=out_specs, check_vma=False)
```

```python
import functools
import math

import jax
import jax.numpy as jnp
from jax import lax
from jax.experimental import pallas as pl
from jax.experimental.pallas import tpu as pltpu
from jax.sharding import PartitionSpec as P

GROUPS = 4
STATE = 128


EPSILON = 1e-05
CTX = ("cx", "cr")


def shifted_up(value, axis, distance):
    size = lax.axis_size(axis)
    pairs = [(source, source + distance) for source in range(size - distance)]
    return lax.ppermute(value, axis, pairs)


def swapped(value, axis):
    return lax.ppermute(value, axis, [(0, 1), (1, 0)])


def span_terms(normed, b_rows, c_rows, step_sizes, rate_row, skip_row):
    count_rows, head_count, head_width = normed.shape
    group_count = b_rows.shape[1]
    per_group = head_count // group_count
    state_root = math.sqrt(b_rows.shape[2])
    log_decay = jnp.cumsum(-step_sizes * rate_row[None, :], axis=0)
    lower_mask = jnp.arange(count_rows)[:, None] >= jnp.arange(count_rows)[None, :]
    intersection = (
        jnp.einsum("tgn,sgn->gts", c_rows, b_rows, precision=lax.Precision.HIGHEST) / state_root
    )
    log_gaps = log_decay.T[:, :, None] - log_decay.T[:, None, :]
    decays = jnp.where(lower_mask[None], jnp.exp(jnp.where(lower_mask[None], log_gaps, 0.0)), 0.0)
    mixing = (
        decays.reshape(group_count, per_group, count_rows, count_rows)
        * intersection[:, None]
        * step_sizes.T.reshape(group_count, per_group, 1, count_rows)
    )
    grouped = normed.reshape(count_rows, group_count, per_group, head_width)
    local_part = jnp.einsum(
        "gkts,sgkp->tgkp", mixing, grouped, precision=lax.Precision.HIGHEST
    ).reshape(count_rows, head_count, head_width)
    tail_weight = jnp.exp(log_decay[-1][None, :] - log_decay) * step_sizes
    weighted = (normed * tail_weight[:, :, None]).reshape(
        count_rows, group_count, per_group, head_width
    )
    ending = jnp.einsum(
        "sgkp,sgn->gkpn", weighted, b_rows, precision=lax.Precision.HIGHEST
    ).reshape(head_count, head_width, b_rows.shape[2])
    return (
        log_decay,
        local_part + skip_row[None, :, None] * normed,
        ending,
        jnp.exp(log_decay[-1]),
    )


def span_inflow(log_decay, c_rows, state_in):
    count_rows, group_count, state_n = c_rows.shape
    head_count, head_width = (state_in.shape[0], state_in.shape[1])
    per_group = head_count // group_count
    state_root = math.sqrt(state_n)
    inflow = jnp.einsum(
        "tgn,gkpn->tgkp",
        c_rows,
        state_in.reshape(group_count, per_group, head_width, state_n),
        precision=lax.Precision.HIGHEST,
    )
    return (
        jnp.exp(log_decay)[:, :, None]
        * inflow.reshape(count_rows, head_count, head_width)
        / state_root
    )


def merge_states(earlier, later):
    return (earlier[0] * later[0], later[0][:, None, None] * earlier[1] + later[1])


def exclusive_scan(decay, state, axis, radix=2):
    place = lax.axis_index(axis)
    size = lax.axis_size(axis)
    incl = (decay, state)
    excl = (jnp.ones_like(decay), jnp.zeros_like(state))
    stride = 1
    while stride < size:
        joined = None
        for step in range(radix - 1, 0, -1):
            distance = step * stride
            if distance >= size:
                continue
            got = jax.tree.map(lambda a: shifted_up(a, axis, distance), incl)
            present = place >= distance
            got = (jnp.where(present, got[0], 1.0), jnp.where(present, got[1], 0.0))
            joined = got if joined is None else merge_states(joined, got)
        excl = merge_states(joined, excl)
        if stride * radix < size:
            incl = merge_states(joined, incl)
        stride *= radix
    return excl


def flash_kernel(place_ref, q_ref, k_ref, v_ref, top_in, total_in, acc_in, top_ref, total_ref, acc_ref, *, row_count, key_block, scale):
    j = pl.program_id(1)
    first = place_ref[0]
    block_start = place_ref[1] + j * key_block

    @pl.when(j == 0)
    def _():
        top_ref[...] = top_in[...]
        total_ref[...] = total_in[...]
        acc_ref[...] = acc_in[...]

    def update(with_mask):
        scores = (
            lax.dot_general(
                q_ref[...], k_ref[...], (((1,), (1,)), ((), ())), preferred_element_type=jnp.float32
            )
            * scale
        )
        if with_mask:
            rows = lax.broadcasted_iota(jnp.int32, (scores.shape[0], 1), 0) % row_count + first
            cols = lax.broadcasted_iota(jnp.int32, (1, scores.shape[1]), 1) + block_start
            allowed = rows >= cols
            scores = jnp.where(allowed, scores, -1e30)
        row_top = top_ref[...]
        new_top = jnp.maximum(row_top, jnp.max(scores, axis=1, keepdims=True))
        raw_weight = jnp.exp(scores - new_top)
        if with_mask:
            raw_weight = jnp.where(allowed, raw_weight, 0.0)
        factor = jnp.exp(row_top - new_top)
        total_ref[...] = total_ref[...] * factor + jnp.sum(raw_weight, axis=1, keepdims=True)
        acc_ref[...] = acc_ref[...] * factor + jnp.dot(
            raw_weight.astype(jnp.bfloat16), v_ref[...], preferred_element_type=jnp.float32
        )
        top_ref[...] = new_top

    present = block_start >= 0

    @pl.when(jnp.logical_and(present, block_start + key_block - 1 <= first))
    def _():
        update(False)

    @pl.when(
        jnp.logical_and(
            jnp.logical_and(present, block_start + key_block - 1 > first),
            block_start <= first + row_count - 1,
        )
    )
    def _():
        update(True)


def flash_step(grouped, both, first_row, key_start, carried, row_count, scale):
    kv_heads, rows, head_width = grouped.shape
    key_count = both.shape[1]
    key_block = math.gcd(key_count, 1024)
    block_total = key_count // key_block

    def block_of(j, place_ref):
        limit = jnp.clip((place_ref[0] + row_count - 1 - place_ref[1]) // key_block, 0, block_total - 1)
        return jnp.where(place_ref[1] < 0, 0, jnp.minimum(j, limit))

    def key_index(h, j, place_ref):
        return (h, block_of(j, place_ref), 0)

    def value_index(h, j, place_ref):
        return (kv_heads + h, block_of(j, place_ref), 0)

    state_spec = lambda width: pl.BlockSpec((None, rows, width), lambda h, j, f: (h, 0, 0))
    return pl.pallas_call(
        functools.partial(flash_kernel, row_count=row_count, key_block=key_block, scale=scale),
        out_shape=(
            jax.ShapeDtypeStruct((kv_heads, rows, 1), jnp.float32),
            jax.ShapeDtypeStruct((kv_heads, rows, 1), jnp.float32),
            jax.ShapeDtypeStruct((kv_heads, rows, head_width), jnp.float32),
        ),
        grid_spec=pltpu.PrefetchScalarGridSpec(
            num_scalar_prefetch=1,
            grid=(kv_heads, block_total),
            in_specs=[
                pl.BlockSpec((None, rows, head_width), lambda h, j, f: (h, 0, 0)),
                pl.BlockSpec((None, key_block, head_width), key_index),
                pl.BlockSpec((None, key_block, head_width), value_index),
                state_spec(1),
                state_spec(1),
                state_spec(head_width),
            ],
            out_specs=[state_spec(1), state_spec(1), state_spec(head_width)],
        ),
        compiler_params=pltpu.CompilerParams(dimension_semantics=("parallel", "arbitrary")),
    )(
        jnp.stack([first_row, key_start]).astype(jnp.int32),
        grouped,
        both,
        both,
        *carried,
    )


def attention_half(queries, keys, values, first_row):
    row_count, q_heads, head_width = queries.shape
    kv_heads = keys.shape[1]
    group_size = q_heads // kv_heads
    score_scale = 1.0 / math.sqrt(head_width)
    rows = group_size * row_count
    grouped = (
        queries.reshape(row_count, kv_heads, group_size, head_width)
        .transpose(1, 2, 0, 3)
        .reshape(kv_heads, rows, head_width)
    )
    both = jnp.concatenate([keys, values], axis=1).transpose(1, 0, 2)
    slab = lax.all_gather(both, "cr", axis=1, tiled=True)
    slab_rows = slab.shape[1]
    outer = lax.axis_index("cx")
    outer_count = lax.axis_size("cx")
    pieces = [shifted_up(slab, "cx", distance) for distance in range(outer_count - 1, 0, -1)]
    carried = (
        jnp.full((kv_heads, rows, 1), -1e30, jnp.float32),
        jnp.zeros((kv_heads, rows, 1), jnp.float32),
        jnp.zeros((kv_heads, rows, head_width), jnp.float32),
    )
    carried = flash_step(grouped, slab, first_row, outer * slab_rows, carried, row_count, score_scale)
    for index, piece in enumerate(reversed(pieces)):
        distance = index + 1
        carried = flash_step(
            grouped, piece, first_row, (outer - distance) * slab_rows, carried, row_count, score_scale
        )
    _, row_total, row_sum = carried
    out = (row_sum / row_total).astype(jnp.bfloat16)
    return (
        out.reshape(kv_heads, group_size, row_count, head_width)
        .transpose(2, 0, 1, 3)
        .reshape(row_count, q_heads * head_width)
    )


def body(queries, keys, values, layer_in, w_bc, w_dt, dt_bias, decay_rate, skip_gain, out_gain):
    seg = lax.axis_index("segment")
    seg_count = lax.axis_size("segment")
    tp = lax.axis_index("tp")
    tp_count = lax.axis_size("tp")
    row_count, q_heads, head_width = queries.shape
    kv_heads = keys.shape[1]
    first_row = lax.axis_index(CTX) * row_count

    q_share = q_heads // seg_count
    kv_share = kv_heads // seg_count
    q_part = lax.dynamic_slice_in_dim(queries, seg * q_share, q_share, 1)
    k_part = lax.dynamic_slice_in_dim(keys, seg * kv_share, kv_share, 1)
    v_part = lax.dynamic_slice_in_dim(values, seg * kv_share, kv_share, 1)
    attended = attention_half(q_part, k_part, v_part, first_row)

    current = layer_in
    channel_count = current.shape[1]
    heads_dev = dt_bias.shape[1]
    state_width = channel_count // heads_dev
    groups_dev = GROUPS // tp_count
    groups_core = groups_dev // seg_count
    heads_core = heads_dev // seg_count
    half_cols = GROUPS * STATE
    wide_rows = current.astype(jnp.float32)
    part_bc = jnp.dot(current, w_bc[0], preferred_element_type=jnp.float32)
    part_dt = jnp.dot(current, w_dt[0], preferred_element_type=jnp.float32)
    part_sq = jnp.sum(wide_rows * wide_rows, axis=1)

    def columns_for(tp_index):
        group_start = (tp_index * groups_dev + seg * groups_core) * STATE
        head_start = tp_index * heads_dev + seg * heads_core
        return jnp.concatenate(
            [
                lax.dynamic_slice_in_dim(part_bc, group_start, groups_core * STATE, 1),
                lax.dynamic_slice_in_dim(part_bc, half_cols + group_start, groups_core * STATE, 1),
                lax.dynamic_slice_in_dim(part_dt, head_start, heads_core, 1),
                part_sq[:, None],
            ],
            axis=1,
        )

    mine = columns_for(tp)
    theirs = columns_for(tp_count - 1 - tp)
    total = mine + swapped(theirs, "tp")
    width_bc = groups_core * STATE
    sum_b = total[:, :width_bc]
    sum_c = total[:, width_bc : 2 * width_bc]
    sum_dt = total[:, 2 * width_bc : 2 * width_bc + heads_core]
    sum_sq = total[:, 2 * width_bc + heads_core]
    inv_rms = lax.rsqrt(sum_sq / (channel_count * tp_count) + EPSILON)
    own_rows = lax.dynamic_slice_in_dim(wide_rows, seg * heads_core * state_width, heads_core * state_width, 1)
    normed = (own_rows * inv_rms[:, None]).reshape(row_count, heads_core, state_width)
    b_rows = (sum_b * inv_rms[:, None]).reshape(row_count, groups_core, STATE)
    c_rows = (sum_c * inv_rms[:, None]).reshape(row_count, groups_core, STATE)
    bias = lax.dynamic_slice_in_dim(dt_bias[0], seg * heads_core, heads_core, 0)
    rate = lax.dynamic_slice_in_dim(decay_rate[0], seg * heads_core, heads_core, 0)
    skip = lax.dynamic_slice_in_dim(skip_gain[0], seg * heads_core, heads_core, 0)
    gain = lax.dynamic_slice_in_dim(out_gain[0], seg * heads_core, heads_core, 0)
    step_sizes = jax.nn.softplus(sum_dt * inv_rms[:, None] + bias[None, :])

    log_decay, local_part, ending, span_decay = span_terms(
        normed, b_rows, c_rows, step_sizes, rate, skip
    )
    _, state_in = exclusive_scan(span_decay, ending, CTX)
    mixed_out = local_part + span_inflow(log_decay, c_rows, state_in)
    power = jnp.mean(mixed_out * mixed_out, axis=2, keepdims=True)
    result = own_rows.reshape(row_count, heads_core, state_width) + gain[None] * mixed_out * lax.rsqrt(
        power + EPSILON
    )
    state_part = result.reshape(row_count, heads_core * state_width).astype(jnp.bfloat16)

    keep_state = seg == 0
    outgoing = jnp.where(keep_state, attended, state_part)
    incoming = swapped(outgoing, "segment")
    first = jnp.where(keep_state, state_part, incoming)
    second = jnp.where(keep_state, incoming, attended)
    return jnp.concatenate([first, second], axis=1)[None]


def solution(mesh):
    ctx_count = mesh.shape["ctx"]
    outer_count = 4 if ctx_count % 4 == 0 else 1
    devices = mesh.devices.reshape(
        mesh.shape["segment"], outer_count, ctx_count // outer_count, mesh.shape["tp"]
    )
    fine = jax.sharding.Mesh(devices, ("segment", "cx", "cr", "tp"))
    in_specs = (
        P(CTX, "tp", None),
        P(CTX, "tp", None),
        P(CTX, "tp", None),
        P(CTX, "tp"),
        P(None, "tp", None),
        P(None, "tp", None),
        P(None, "tp"),
        P(None, "tp"),
        P(None, "tp"),
        P(None, "tp", None),
    )
    out_specs = P("segment", CTX, "tp")
    return jax.shard_map(body, mesh=fine, in_specs=in_specs, out_specs=out_specs, check_vma=False)
```

```python
import functools
import math

import jax
import jax.numpy as jnp
from jax import lax
from jax.experimental import pallas as pl
from jax.experimental.pallas import tpu as pltpu
from jax.sharding import PartitionSpec as P

GROUPS = 4
STATE = 128


EPSILON = 1e-05
CTX = ("cx", "cz", "cy")


def shifted_up(value, axis, distance):
    size = lax.axis_size(axis)
    pairs = [(source, source + distance) for source in range(size - distance)]
    return lax.ppermute(value, axis, pairs)


def swapped(value, axis):
    return lax.ppermute(value, axis, [(0, 1), (1, 0)])


def span_terms(normed, b_rows, c_rows, step_sizes, rate_row, skip_row):
    count_rows, head_count, head_width = normed.shape
    group_count = b_rows.shape[1]
    per_group = head_count // group_count
    state_root = math.sqrt(b_rows.shape[2])
    log_decay = jnp.cumsum(-step_sizes * rate_row[None, :], axis=0)
    lower_mask = jnp.arange(count_rows)[:, None] >= jnp.arange(count_rows)[None, :]
    intersection = (
        jnp.einsum("tgn,sgn->gts", c_rows, b_rows, precision=lax.Precision.HIGHEST) / state_root
    )
    log_gaps = log_decay.T[:, :, None] - log_decay.T[:, None, :]
    decays = jnp.where(lower_mask[None], jnp.exp(jnp.where(lower_mask[None], log_gaps, 0.0)), 0.0)
    mixing = (
        decays.reshape(group_count, per_group, count_rows, count_rows)
        * intersection[:, None]
        * step_sizes.T.reshape(group_count, per_group, 1, count_rows)
    )
    grouped = normed.reshape(count_rows, group_count, per_group, head_width)
    local_part = jnp.einsum(
        "gkts,sgkp->tgkp", mixing, grouped, precision=lax.Precision.HIGHEST
    ).reshape(count_rows, head_count, head_width)
    tail_weight = jnp.exp(log_decay[-1][None, :] - log_decay) * step_sizes
    weighted = (normed * tail_weight[:, :, None]).reshape(
        count_rows, group_count, per_group, head_width
    )
    ending = jnp.einsum(
        "sgkp,sgn->gkpn", weighted, b_rows, precision=lax.Precision.HIGHEST
    ).reshape(head_count, head_width, b_rows.shape[2])
    return (
        log_decay,
        local_part + skip_row[None, :, None] * normed,
        ending,
        jnp.exp(log_decay[-1]),
    )


def span_inflow(log_decay, c_rows, state_in):
    count_rows, group_count, state_n = c_rows.shape
    head_count, head_width = (state_in.shape[0], state_in.shape[1])
    per_group = head_count // group_count
    state_root = math.sqrt(state_n)
    inflow = jnp.einsum(
        "tgn,gkpn->tgkp",
        c_rows,
        state_in.reshape(group_count, per_group, head_width, state_n),
        precision=lax.Precision.HIGHEST,
    )
    return (
        jnp.exp(log_decay)[:, :, None]
        * inflow.reshape(count_rows, head_count, head_width)
        / state_root
    )


def merge_states(earlier, later):
    return (earlier[0] * later[0], later[0][:, None, None] * earlier[1] + later[1])


def exclusive_scan(decay, state, axis, radix=2):
    place = lax.axis_index(axis)
    size = lax.axis_size(axis)
    incl = (decay, state)
    excl = (jnp.ones_like(decay), jnp.zeros_like(state))
    stride = 1
    while stride < size:
        joined = None
        for step in range(radix - 1, 0, -1):
            distance = step * stride
            if distance >= size:
                continue
            got = jax.tree.map(lambda a: shifted_up(a, axis, distance), incl)
            present = place >= distance
            got = (jnp.where(present, got[0], 1.0), jnp.where(present, got[1], 0.0))
            joined = got if joined is None else merge_states(joined, got)
        excl = merge_states(joined, excl)
        if stride * radix < size:
            incl = merge_states(joined, incl)
        stride *= radix
    return excl


def flash_kernel(first_ref, q_ref, k_ref, v_ref, o_ref, top_ref, total_ref, acc_ref, *, row_count, key_block, scale):
    j = pl.program_id(1)
    first = first_ref[0]
    block_start = j * key_block

    @pl.when(j == 0)
    def _():
        top_ref[...] = jnp.full(top_ref.shape, -1e30, jnp.float32)
        total_ref[...] = jnp.zeros(total_ref.shape, jnp.float32)
        acc_ref[...] = jnp.zeros(acc_ref.shape, jnp.float32)

    def update(with_mask):
        scores = (
            lax.dot_general(
                q_ref[...], k_ref[...], (((1,), (1,)), ((), ())), preferred_element_type=jnp.float32
            )
            * scale
        )
        if with_mask:
            rows = lax.broadcasted_iota(jnp.int32, (scores.shape[0], 1), 0) % row_count + first
            cols = lax.broadcasted_iota(jnp.int32, (1, scores.shape[1]), 1) + block_start
            allowed = rows >= cols
            scores = jnp.where(allowed, scores, -1e30)
        row_top = top_ref[...]
        new_top = jnp.maximum(row_top, jnp.max(scores, axis=1, keepdims=True))
        raw_weight = jnp.exp(scores - new_top)
        if with_mask:
            raw_weight = jnp.where(allowed, raw_weight, 0.0)
        factor = jnp.exp(row_top - new_top)
        total_ref[...] = total_ref[...] * factor + jnp.sum(raw_weight, axis=1, keepdims=True)
        acc_ref[...] = acc_ref[...] * factor + jnp.dot(
            raw_weight.astype(jnp.bfloat16), v_ref[...], preferred_element_type=jnp.float32
        )
        top_ref[...] = new_top

    @pl.when(block_start + key_block - 1 <= first)
    def _():
        update(False)

    @pl.when(
        jnp.logical_and(block_start + key_block - 1 > first, block_start <= first + row_count - 1)
    )
    def _():
        update(True)

    @pl.when(j == pl.num_programs(1) - 1)
    def _():
        o_ref[...] = (acc_ref[...] / total_ref[...]).astype(o_ref.dtype)


def attention_half(queries, keys, values, first_row):
    row_count, q_heads, head_width = queries.shape
    kv_heads = keys.shape[1]
    group_size = q_heads // kv_heads
    score_scale = 1.0 / math.sqrt(head_width)
    grouped = (
        queries.reshape(row_count, kv_heads, group_size, head_width)
        .transpose(1, 2, 0, 3)
        .reshape(kv_heads, group_size * row_count, head_width)
    )
    both = jnp.concatenate([keys, values], axis=1).transpose(1, 0, 2)
    both_all = both
    for axis in reversed(CTX):
        both_all = lax.all_gather(both_all, axis, axis=1, tiled=True)
    key_count = both_all.shape[1]
    key_block = math.gcd(key_count, 1024)
    rows = group_size * row_count

    def key_index(h, j, first_ref):
        return (h, jnp.minimum(j, (first_ref[0] + row_count - 1) // key_block), 0)

    def value_index(h, j, first_ref):
        return (kv_heads + h, jnp.minimum(j, (first_ref[0] + row_count - 1) // key_block), 0)

    out = pl.pallas_call(
        functools.partial(flash_kernel, row_count=row_count, key_block=key_block, scale=score_scale),
        out_shape=jax.ShapeDtypeStruct((kv_heads, rows, head_width), jnp.bfloat16),
        grid_spec=pltpu.PrefetchScalarGridSpec(
            num_scalar_prefetch=1,
            grid=(kv_heads, key_count // key_block),
            in_specs=[
                pl.BlockSpec((None, rows, head_width), lambda h, j, f: (h, 0, 0)),
                pl.BlockSpec((None, key_block, head_width), key_index),
                pl.BlockSpec((None, key_block, head_width), value_index),
            ],
            out_specs=pl.BlockSpec((None, rows, head_width), lambda h, j, f: (h, 0, 0)),
            scratch_shapes=[
                pltpu.VMEM((rows, 1), jnp.float32),
                pltpu.VMEM((rows, 1), jnp.float32),
                pltpu.VMEM((rows, head_width), jnp.float32),
            ],
        ),
        compiler_params=pltpu.CompilerParams(dimension_semantics=("parallel", "arbitrary")),
    )(jnp.reshape(first_row, (1,)).astype(jnp.int32), grouped, both_all, both_all)
    return (
        out.reshape(kv_heads, group_size, row_count, head_width)
        .transpose(2, 0, 1, 3)
        .reshape(row_count, q_heads * head_width)
    )


def body(queries, keys, values, layer_in, w_bc, w_dt, dt_bias, decay_rate, skip_gain, out_gain):
    seg = lax.axis_index("segment")
    seg_count = lax.axis_size("segment")
    tp = lax.axis_index("tp")
    tp_count = lax.axis_size("tp")
    row_count, q_heads, head_width = queries.shape
    kv_heads = keys.shape[1]
    first_row = lax.axis_index(CTX) * row_count

    q_share = q_heads // seg_count
    kv_share = kv_heads // seg_count
    q_part = lax.dynamic_slice_in_dim(queries, seg * q_share, q_share, 1)
    k_part = lax.dynamic_slice_in_dim(keys, seg * kv_share, kv_share, 1)
    v_part = lax.dynamic_slice_in_dim(values, seg * kv_share, kv_share, 1)
    attended = attention_half(q_part, k_part, v_part, first_row)

    current = layer_in
    channel_count = current.shape[1]
    heads_dev = dt_bias.shape[1]
    state_width = channel_count // heads_dev
    groups_dev = GROUPS // tp_count
    groups_core = groups_dev // seg_count
    heads_core = heads_dev // seg_count
    half_cols = GROUPS * STATE
    wide_rows = current.astype(jnp.float32)
    part_bc = jnp.dot(current, w_bc[0], preferred_element_type=jnp.float32)
    part_dt = jnp.dot(current, w_dt[0], preferred_element_type=jnp.float32)
    part_sq = jnp.sum(wide_rows * wide_rows, axis=1)

    def columns_for(tp_index):
        group_start = (tp_index * groups_dev + seg * groups_core) * STATE
        head_start = tp_index * heads_dev + seg * heads_core
        return jnp.concatenate(
            [
                lax.dynamic_slice_in_dim(part_bc, group_start, groups_core * STATE, 1),
                lax.dynamic_slice_in_dim(part_bc, half_cols + group_start, groups_core * STATE, 1),
                lax.dynamic_slice_in_dim(part_dt, head_start, heads_core, 1),
                part_sq[:, None],
            ],
            axis=1,
        )

    mine = columns_for(tp)
    theirs = columns_for(tp_count - 1 - tp)
    total = mine + swapped(theirs, "tp")
    width_bc = groups_core * STATE
    sum_b = total[:, :width_bc]
    sum_c = total[:, width_bc : 2 * width_bc]
    sum_dt = total[:, 2 * width_bc : 2 * width_bc + heads_core]
    sum_sq = total[:, 2 * width_bc + heads_core]
    inv_rms = lax.rsqrt(sum_sq / (channel_count * tp_count) + EPSILON)
    own_rows = lax.dynamic_slice_in_dim(wide_rows, seg * heads_core * state_width, heads_core * state_width, 1)
    normed = (own_rows * inv_rms[:, None]).reshape(row_count, heads_core, state_width)
    b_rows = (sum_b * inv_rms[:, None]).reshape(row_count, groups_core, STATE)
    c_rows = (sum_c * inv_rms[:, None]).reshape(row_count, groups_core, STATE)
    bias = lax.dynamic_slice_in_dim(dt_bias[0], seg * heads_core, heads_core, 0)
    rate = lax.dynamic_slice_in_dim(decay_rate[0], seg * heads_core, heads_core, 0)
    skip = lax.dynamic_slice_in_dim(skip_gain[0], seg * heads_core, heads_core, 0)
    gain = lax.dynamic_slice_in_dim(out_gain[0], seg * heads_core, heads_core, 0)
    step_sizes = jax.nn.softplus(sum_dt * inv_rms[:, None] + bias[None, :])

    log_decay, local_part, ending, span_decay = span_terms(
        normed, b_rows, c_rows, step_sizes, rate, skip
    )
    _, state_in = exclusive_scan(span_decay, ending, CTX)
    mixed_out = local_part + span_inflow(log_decay, c_rows, state_in)
    power = jnp.mean(mixed_out * mixed_out, axis=2, keepdims=True)
    result = own_rows.reshape(row_count, heads_core, state_width) + gain[None] * mixed_out * lax.rsqrt(
        power + EPSILON
    )
    state_part = result.reshape(row_count, heads_core * state_width).astype(jnp.bfloat16)

    keep_state = seg == 0
    outgoing = jnp.where(keep_state, attended, state_part)
    incoming = swapped(outgoing, "segment")
    first = jnp.where(keep_state, state_part, incoming)
    second = jnp.where(keep_state, incoming, attended)
    return jnp.concatenate([first, second], axis=1)[None]


def solution(mesh):
    ctx_count = mesh.shape["ctx"]
    outer_count = 4 if ctx_count % 4 == 0 else 1
    inner_count = 2 if (ctx_count // outer_count) % 2 == 0 else 1
    devices = mesh.devices.reshape(
        mesh.shape["segment"],
        outer_count,
        ctx_count // (outer_count * inner_count),
        inner_count,
        mesh.shape["tp"],
    )
    fine = jax.sharding.Mesh(devices, ("segment", "cx", "cz", "cy", "tp"))
    in_specs = (
        P(CTX, "tp", None),
        P(CTX, "tp", None),
        P(CTX, "tp", None),
        P(CTX, "tp"),
        P(None, "tp", None),
        P(None, "tp", None),
        P(None, "tp"),
        P(None, "tp"),
        P(None, "tp"),
        P(None, "tp", None),
    )
    out_specs = P("segment", CTX, "tp")
    return jax.shard_map(body, mesh=fine, in_specs=in_specs, out_specs=out_specs, check_vma=False)
```

```python
import functools
import math

import jax
import jax.numpy as jnp
from jax import lax
from jax.experimental import pallas as pl
from jax.experimental.pallas import tpu as pltpu
from jax.sharding import PartitionSpec as P

GROUPS = 4
STATE = 128


EPSILON = 1e-05


def shifted_up(value, axis, distance):
    size = lax.axis_size(axis)
    pairs = [(source, source + distance) for source in range(size - distance)]
    return lax.ppermute(value, axis, pairs)


def swapped(value, axis):
    return lax.ppermute(value, axis, [(0, 1), (1, 0)])


def span_terms(normed, b_rows, c_rows, step_sizes, rate_row, skip_row):
    count_rows, head_count, head_width = normed.shape
    group_count = b_rows.shape[1]
    per_group = head_count // group_count
    state_root = math.sqrt(b_rows.shape[2])
    log_decay = jnp.cumsum(-step_sizes * rate_row[None, :], axis=0)
    lower_mask = jnp.arange(count_rows)[:, None] >= jnp.arange(count_rows)[None, :]
    intersection = (
        jnp.einsum("tgn,sgn->gts", c_rows, b_rows, precision=lax.Precision.HIGHEST) / state_root
    )
    log_gaps = log_decay.T[:, :, None] - log_decay.T[:, None, :]
    decays = jnp.where(lower_mask[None], jnp.exp(jnp.where(lower_mask[None], log_gaps, 0.0)), 0.0)
    mixing = (
        decays.reshape(group_count, per_group, count_rows, count_rows)
        * intersection[:, None]
        * step_sizes.T.reshape(group_count, per_group, 1, count_rows)
    )
    grouped = normed.reshape(count_rows, group_count, per_group, head_width)
    local_part = jnp.einsum(
        "gkts,sgkp->tgkp", mixing, grouped, precision=lax.Precision.HIGHEST
    ).reshape(count_rows, head_count, head_width)
    tail_weight = jnp.exp(log_decay[-1][None, :] - log_decay) * step_sizes
    weighted = (normed * tail_weight[:, :, None]).reshape(
        count_rows, group_count, per_group, head_width
    )
    ending = jnp.einsum(
        "sgkp,sgn->gkpn", weighted, b_rows, precision=lax.Precision.HIGHEST
    ).reshape(head_count, head_width, b_rows.shape[2])
    return (
        log_decay,
        local_part + skip_row[None, :, None] * normed,
        ending,
        jnp.exp(log_decay[-1]),
    )


def span_inflow(log_decay, c_rows, state_in):
    count_rows, group_count, state_n = c_rows.shape
    head_count, head_width = (state_in.shape[0], state_in.shape[1])
    per_group = head_count // group_count
    state_root = math.sqrt(state_n)
    inflow = jnp.einsum(
        "tgn,gkpn->tgkp",
        c_rows,
        state_in.reshape(group_count, per_group, head_width, state_n),
        precision=lax.Precision.HIGHEST,
    )
    return (
        jnp.exp(log_decay)[:, :, None]
        * inflow.reshape(count_rows, head_count, head_width)
        / state_root
    )


def merge_states(earlier, later):
    return (earlier[0] * later[0], later[0][:, None, None] * earlier[1] + later[1])


def exclusive_scan(decay, state, axis, radix=2):
    place = lax.axis_index(axis)
    size = lax.axis_size(axis)
    incl = (decay, state)
    excl = (jnp.ones_like(decay), jnp.zeros_like(state))
    stride = 1
    while stride < size:
        joined = None
        for step in range(radix - 1, 0, -1):
            distance = step * stride
            if distance >= size:
                continue
            got = jax.tree.map(lambda a: shifted_up(a, axis, distance), incl)
            present = place >= distance
            got = (jnp.where(present, got[0], 1.0), jnp.where(present, got[1], 0.0))
            joined = got if joined is None else merge_states(joined, got)
        excl = merge_states(joined, excl)
        if stride * radix < size:
            incl = merge_states(joined, incl)
        stride *= radix
    return excl


def flash_kernel(first_ref, q_ref, k_ref, v_ref, o_ref, top_ref, total_ref, acc_ref, *, row_count, key_block, scale):
    j = pl.program_id(1)
    first = first_ref[0]
    block_start = j * key_block

    @pl.when(j == 0)
    def _():
        top_ref[...] = jnp.full(top_ref.shape, -1e30, jnp.float32)
        total_ref[...] = jnp.zeros(total_ref.shape, jnp.float32)
        acc_ref[...] = jnp.zeros(acc_ref.shape, jnp.float32)

    def update(with_mask):
        scores = (
            lax.dot_general(
                q_ref[...], k_ref[...], (((1,), (1,)), ((), ())), preferred_element_type=jnp.float32
            )
            * scale
        )
        if with_mask:
            rows = lax.broadcasted_iota(jnp.int32, (scores.shape[0], 1), 0) % row_count + first
            cols = lax.broadcasted_iota(jnp.int32, (1, scores.shape[1]), 1) + block_start
            allowed = rows >= cols
            scores = jnp.where(allowed, scores, -1e30)
        row_top = top_ref[...]
        new_top = jnp.maximum(row_top, jnp.max(scores, axis=1, keepdims=True))
        raw_weight = jnp.exp(scores - new_top)
        if with_mask:
            raw_weight = jnp.where(allowed, raw_weight, 0.0)
        factor = jnp.exp(row_top - new_top)
        total_ref[...] = total_ref[...] * factor + jnp.sum(raw_weight, axis=1, keepdims=True)
        acc_ref[...] = acc_ref[...] * factor + jnp.dot(
            raw_weight.astype(jnp.bfloat16), v_ref[...], preferred_element_type=jnp.float32
        )
        top_ref[...] = new_top

    @pl.when(block_start + key_block - 1 <= first)
    def _():
        update(False)

    @pl.when(
        jnp.logical_and(block_start + key_block - 1 > first, block_start <= first + row_count - 1)
    )
    def _():
        update(True)

    @pl.when(j == pl.num_programs(1) - 1)
    def _():
        o_ref[...] = (acc_ref[...] / total_ref[...]).astype(o_ref.dtype)


def attention_half(queries, keys, values, first_row):
    row_count, q_heads, head_width = queries.shape
    kv_heads = keys.shape[1]
    group_size = q_heads // kv_heads
    score_scale = 1.0 / math.sqrt(head_width)
    grouped = (
        queries.reshape(row_count, kv_heads, group_size, head_width)
        .transpose(1, 2, 0, 3)
        .reshape(kv_heads, group_size * row_count, head_width)
    )
    both = jnp.concatenate([keys, values], axis=1).transpose(1, 0, 2)
    both_all = lax.all_gather(both, "ctx", axis=1, tiled=True)
    key_count = both_all.shape[1]
    key_block = math.gcd(key_count, 2048)
    rows = group_size * row_count

    def key_index(h, j, first_ref):
        return (h, jnp.minimum(j, (first_ref[0] + row_count - 1) // key_block), 0)

    def value_index(h, j, first_ref):
        return (kv_heads + h, jnp.minimum(j, (first_ref[0] + row_count - 1) // key_block), 0)

    out = pl.pallas_call(
        functools.partial(flash_kernel, row_count=row_count, key_block=key_block, scale=score_scale),
        out_shape=jax.ShapeDtypeStruct((kv_heads, rows, head_width), jnp.bfloat16),
        grid_spec=pltpu.PrefetchScalarGridSpec(
            num_scalar_prefetch=1,
            grid=(kv_heads, key_count // key_block),
            in_specs=[
                pl.BlockSpec((None, rows, head_width), lambda h, j, f: (h, 0, 0)),
                pl.BlockSpec((None, key_block, head_width), key_index),
                pl.BlockSpec((None, key_block, head_width), value_index),
            ],
            out_specs=pl.BlockSpec((None, rows, head_width), lambda h, j, f: (h, 0, 0)),
            scratch_shapes=[
                pltpu.VMEM((rows, 1), jnp.float32),
                pltpu.VMEM((rows, 1), jnp.float32),
                pltpu.VMEM((rows, head_width), jnp.float32),
            ],
        ),
        compiler_params=pltpu.CompilerParams(dimension_semantics=("parallel", "arbitrary")),
    )(jnp.reshape(first_row, (1,)).astype(jnp.int32), grouped, both_all, both_all)
    return (
        out.reshape(kv_heads, group_size, row_count, head_width)
        .transpose(2, 0, 1, 3)
        .reshape(row_count, q_heads * head_width)
    )


def body(queries, keys, values, layer_in, w_bc, w_dt, dt_bias, decay_rate, skip_gain, out_gain):
    seg = lax.axis_index("segment")
    seg_count = lax.axis_size("segment")
    tp = lax.axis_index("tp")
    tp_count = lax.axis_size("tp")
    row_count, q_heads, head_width = queries.shape
    kv_heads = keys.shape[1]
    first_row = lax.axis_index("ctx") * row_count

    q_share = q_heads // seg_count
    kv_share = kv_heads // seg_count
    q_part = lax.dynamic_slice_in_dim(queries, seg * q_share, q_share, 1)
    k_part = lax.dynamic_slice_in_dim(keys, seg * kv_share, kv_share, 1)
    v_part = lax.dynamic_slice_in_dim(values, seg * kv_share, kv_share, 1)
    attended = attention_half(q_part, k_part, v_part, first_row)

    current = layer_in
    channel_count = current.shape[1]
    heads_dev = dt_bias.shape[1]
    state_width = channel_count // heads_dev
    groups_dev = GROUPS // tp_count
    groups_core = groups_dev // seg_count
    heads_core = heads_dev // seg_count
    half_cols = GROUPS * STATE
    wide_rows = current.astype(jnp.float32)
    part_bc = jnp.dot(current, w_bc[0], preferred_element_type=jnp.float32)
    part_dt = jnp.dot(current, w_dt[0], preferred_element_type=jnp.float32)
    part_sq = jnp.sum(wide_rows * wide_rows, axis=1)

    def columns_for(tp_index):
        group_start = (tp_index * groups_dev + seg * groups_core) * STATE
        head_start = tp_index * heads_dev + seg * heads_core
        return jnp.concatenate(
            [
                lax.dynamic_slice_in_dim(part_bc, group_start, groups_core * STATE, 1),
                lax.dynamic_slice_in_dim(part_bc, half_cols + group_start, groups_core * STATE, 1),
                lax.dynamic_slice_in_dim(part_dt, head_start, heads_core, 1),
                part_sq[:, None],
            ],
            axis=1,
        )

    mine = columns_for(tp)
    theirs = columns_for(tp_count - 1 - tp)
    total = mine + swapped(theirs, "tp")
    width_bc = groups_core * STATE
    sum_b = total[:, :width_bc]
    sum_c = total[:, width_bc : 2 * width_bc]
    sum_dt = total[:, 2 * width_bc : 2 * width_bc + heads_core]
    sum_sq = total[:, 2 * width_bc + heads_core]
    inv_rms = lax.rsqrt(sum_sq / (channel_count * tp_count) + EPSILON)
    own_rows = lax.dynamic_slice_in_dim(wide_rows, seg * heads_core * state_width, heads_core * state_width, 1)
    normed = (own_rows * inv_rms[:, None]).reshape(row_count, heads_core, state_width)
    b_rows = (sum_b * inv_rms[:, None]).reshape(row_count, groups_core, STATE)
    c_rows = (sum_c * inv_rms[:, None]).reshape(row_count, groups_core, STATE)
    bias = lax.dynamic_slice_in_dim(dt_bias[0], seg * heads_core, heads_core, 0)
    rate = lax.dynamic_slice_in_dim(decay_rate[0], seg * heads_core, heads_core, 0)
    skip = lax.dynamic_slice_in_dim(skip_gain[0], seg * heads_core, heads_core, 0)
    gain = lax.dynamic_slice_in_dim(out_gain[0], seg * heads_core, heads_core, 0)
    step_sizes = jax.nn.softplus(sum_dt * inv_rms[:, None] + bias[None, :])

    log_decay, local_part, ending, span_decay = span_terms(
        normed, b_rows, c_rows, step_sizes, rate, skip
    )
    _, state_in = exclusive_scan(span_decay, ending, "ctx")
    mixed_out = local_part + span_inflow(log_decay, c_rows, state_in)
    power = jnp.mean(mixed_out * mixed_out, axis=2, keepdims=True)
    result = own_rows.reshape(row_count, heads_core, state_width) + gain[None] * mixed_out * lax.rsqrt(
        power + EPSILON
    )
    state_part = result.reshape(row_count, heads_core * state_width).astype(jnp.bfloat16)

    keep_state = seg == 0
    state_in_half = lax.ppermute(state_part, "segment", [(1, 0)])
    attended_in_half = lax.ppermute(attended, "segment", [(0, 1)])
    first = jnp.where(keep_state, state_part, attended_in_half)
    second = jnp.where(keep_state, state_in_half, attended)
    return jnp.concatenate([first, second], axis=1)[None]


def solution(mesh):
    in_specs = (
        P("ctx", "tp", None),
        P("ctx", "tp", None),
        P("ctx", "tp", None),
        P("ctx", "tp"),
        P(None, "tp", None),
        P(None, "tp", None),
        P(None, "tp"),
        P(None, "tp"),
        P(None, "tp"),
        P(None, "tp", None),
    )
    out_specs = P("segment", "ctx", "tp")
    return jax.shard_map(body, mesh=mesh, in_specs=in_specs, out_specs=out_specs, check_vma=False)
```

```python
import functools
import math

import jax
import jax.numpy as jnp
from jax import lax
from jax.experimental import pallas as pl
from jax.experimental.pallas import tpu as pltpu
from jax.sharding import PartitionSpec as P

GROUPS = 4
STATE = 128


EPSILON = 1e-05


def shifted_up(value, axis, distance):
    size = lax.axis_size(axis)
    pairs = [(source, source + distance) for source in range(size - distance)]
    return lax.ppermute(value, axis, pairs)


def swapped(value, axis):
    return lax.ppermute(value, axis, [(0, 1), (1, 0)])


def span_terms(normed, b_rows, c_rows, step_sizes, rate_row, skip_row):
    count_rows, head_count, head_width = normed.shape
    group_count = b_rows.shape[1]
    per_group = head_count // group_count
    state_root = math.sqrt(b_rows.shape[2])
    log_decay = jnp.cumsum(-step_sizes * rate_row[None, :], axis=0)
    lower_mask = jnp.arange(count_rows)[:, None] >= jnp.arange(count_rows)[None, :]
    intersection = (
        jnp.einsum("tgn,sgn->gts", c_rows, b_rows, precision=lax.Precision.HIGHEST) / state_root
    )
    log_gaps = log_decay.T[:, :, None] - log_decay.T[:, None, :]
    decays = jnp.where(lower_mask[None], jnp.exp(jnp.where(lower_mask[None], log_gaps, 0.0)), 0.0)
    mixing = (
        decays.reshape(group_count, per_group, count_rows, count_rows)
        * intersection[:, None]
        * step_sizes.T.reshape(group_count, per_group, 1, count_rows)
    )
    grouped = normed.reshape(count_rows, group_count, per_group, head_width)
    local_part = jnp.einsum(
        "gkts,sgkp->tgkp", mixing, grouped, precision=lax.Precision.HIGHEST
    ).reshape(count_rows, head_count, head_width)
    tail_weight = jnp.exp(log_decay[-1][None, :] - log_decay) * step_sizes
    weighted = (normed * tail_weight[:, :, None]).reshape(
        count_rows, group_count, per_group, head_width
    )
    ending = jnp.einsum(
        "sgkp,sgn->gkpn", weighted, b_rows, precision=lax.Precision.HIGHEST
    ).reshape(head_count, head_width, b_rows.shape[2])
    return (
        log_decay,
        local_part + skip_row[None, :, None] * normed,
        ending,
        jnp.exp(log_decay[-1]),
    )


def span_inflow(log_decay, c_rows, state_in):
    count_rows, group_count, state_n = c_rows.shape
    head_count, head_width = (state_in.shape[0], state_in.shape[1])
    per_group = head_count // group_count
    state_root = math.sqrt(state_n)
    inflow = jnp.einsum(
        "tgn,gkpn->tgkp",
        c_rows,
        state_in.reshape(group_count, per_group, head_width, state_n),
        precision=lax.Precision.HIGHEST,
    )
    return (
        jnp.exp(log_decay)[:, :, None]
        * inflow.reshape(count_rows, head_count, head_width)
        / state_root
    )


def merge_states(earlier, later):
    return (earlier[0] * later[0], later[0][:, None, None] * earlier[1] + later[1])


def exclusive_scan(decay, state, axis, radix=2):
    place = lax.axis_index(axis)
    size = lax.axis_size(axis)
    incl = (decay, state)
    excl = (jnp.ones_like(decay), jnp.zeros_like(state))
    stride = 1
    while stride < size:
        joined = None
        for step in range(radix - 1, 0, -1):
            distance = step * stride
            if distance >= size:
                continue
            got = jax.tree.map(lambda a: shifted_up(a, axis, distance), incl)
            present = place >= distance
            got = (jnp.where(present, got[0], 1.0), jnp.where(present, got[1], 0.0))
            joined = got if joined is None else merge_states(joined, got)
        excl = merge_states(joined, excl)
        if stride * radix < size:
            incl = merge_states(joined, incl)
        stride *= radix
    return excl


def flash_kernel(first_ref, q_ref, k_ref, v_ref, o_ref, top_ref, total_ref, acc_ref, *, row_count, key_block, scale):
    j = pl.program_id(1)
    first = first_ref[0]
    block_start = j * key_block

    @pl.when(j == 0)
    def _():
        top_ref[...] = jnp.full(top_ref.shape, -1e30, jnp.float32)
        total_ref[...] = jnp.zeros(total_ref.shape, jnp.float32)
        acc_ref[...] = jnp.zeros(acc_ref.shape, jnp.float32)

    def update(with_mask):
        scores = (
            lax.dot_general(
                q_ref[...], k_ref[...], (((1,), (1,)), ((), ())), preferred_element_type=jnp.float32
            )
            * scale
        )
        if with_mask:
            rows = lax.broadcasted_iota(jnp.int32, (scores.shape[0], 1), 0) % row_count + first
            cols = lax.broadcasted_iota(jnp.int32, (1, scores.shape[1]), 1) + block_start
            allowed = rows >= cols
            scores = jnp.where(allowed, scores, -1e30)
        row_top = top_ref[...]
        new_top = jnp.maximum(row_top, jnp.max(scores, axis=1, keepdims=True))
        raw_weight = jnp.exp(scores - new_top)
        if with_mask:
            raw_weight = jnp.where(allowed, raw_weight, 0.0)
        factor = jnp.exp(row_top - new_top)
        total_ref[...] = total_ref[...] * factor + jnp.sum(raw_weight, axis=1, keepdims=True)
        acc_ref[...] = acc_ref[...] * factor + jnp.dot(
            raw_weight.astype(jnp.bfloat16), v_ref[...], preferred_element_type=jnp.float32
        )
        top_ref[...] = new_top

    @pl.when(block_start + key_block - 1 <= first)
    def _():
        update(False)

    @pl.when(
        jnp.logical_and(block_start + key_block - 1 > first, block_start <= first + row_count - 1)
    )
    def _():
        update(True)

    @pl.when(j == pl.num_programs(1) - 1)
    def _():
        o_ref[...] = (acc_ref[...] / total_ref[...]).astype(o_ref.dtype)


def attention_half(queries, keys, values, first_row):
    row_count, q_heads, head_width = queries.shape
    kv_heads = keys.shape[1]
    group_size = q_heads // kv_heads
    score_scale = 1.0 / math.sqrt(head_width)
    grouped = (
        queries.reshape(row_count, kv_heads, group_size, head_width)
        .transpose(1, 2, 0, 3)
        .reshape(kv_heads, group_size * row_count, head_width)
    )
    both = jnp.concatenate([keys, values], axis=1).transpose(1, 0, 2)
    both_all = lax.all_gather(both, "ctx", axis=1, tiled=True)
    key_count = both_all.shape[1]
    key_block = math.gcd(key_count, 4096)
    rows = group_size * row_count

    def key_index(h, j, first_ref):
        return (h, jnp.minimum(j, (first_ref[0] + row_count - 1) // key_block), 0)

    def value_index(h, j, first_ref):
        return (kv_heads + h, jnp.minimum(j, (first_ref[0] + row_count - 1) // key_block), 0)

    out = pl.pallas_call(
        functools.partial(flash_kernel, row_count=row_count, key_block=key_block, scale=score_scale),
        out_shape=jax.ShapeDtypeStruct((kv_heads, rows, head_width), jnp.bfloat16),
        grid_spec=pltpu.PrefetchScalarGridSpec(
            num_scalar_prefetch=1,
            grid=(kv_heads, key_count // key_block),
            in_specs=[
                pl.BlockSpec((None, rows, head_width), lambda h, j, f: (h, 0, 0)),
                pl.BlockSpec((None, key_block, head_width), key_index),
                pl.BlockSpec((None, key_block, head_width), value_index),
            ],
            out_specs=pl.BlockSpec((None, rows, head_width), lambda h, j, f: (h, 0, 0)),
            scratch_shapes=[
                pltpu.VMEM((rows, 1), jnp.float32),
                pltpu.VMEM((rows, 1), jnp.float32),
                pltpu.VMEM((rows, head_width), jnp.float32),
            ],
        ),
        compiler_params=pltpu.CompilerParams(dimension_semantics=("parallel", "arbitrary")),
    )(jnp.reshape(first_row, (1,)).astype(jnp.int32), grouped, both_all, both_all)
    return (
        out.reshape(kv_heads, group_size, row_count, head_width)
        .transpose(2, 0, 1, 3)
        .reshape(row_count, q_heads * head_width)
    )


def body(queries, keys, values, layer_in, w_bc, w_dt, dt_bias, decay_rate, skip_gain, out_gain):
    seg = lax.axis_index("segment")
    seg_count = lax.axis_size("segment")
    tp = lax.axis_index("tp")
    tp_count = lax.axis_size("tp")
    row_count, q_heads, head_width = queries.shape
    kv_heads = keys.shape[1]
    first_row = lax.axis_index("ctx") * row_count

    q_share = q_heads // seg_count
    kv_share = kv_heads // seg_count
    q_part = lax.dynamic_slice_in_dim(queries, seg * q_share, q_share, 1)
    k_part = lax.dynamic_slice_in_dim(keys, seg * kv_share, kv_share, 1)
    v_part = lax.dynamic_slice_in_dim(values, seg * kv_share, kv_share, 1)
    attended = attention_half(q_part, k_part, v_part, first_row)

    current = layer_in
    channel_count = current.shape[1]
    heads_dev = dt_bias.shape[1]
    state_width = channel_count // heads_dev
    groups_dev = GROUPS // tp_count
    groups_core = groups_dev // seg_count
    heads_core = heads_dev // seg_count
    half_cols = GROUPS * STATE
    wide_rows = current.astype(jnp.float32)
    part_bc = jnp.dot(current, w_bc[0], preferred_element_type=jnp.float32)
    part_dt = jnp.dot(current, w_dt[0], preferred_element_type=jnp.float32)
    part_sq = jnp.sum(wide_rows * wide_rows, axis=1)

    def columns_for(tp_index):
        group_start = (tp_index * groups_dev + seg * groups_core) * STATE
        head_start = tp_index * heads_dev + seg * heads_core
        return jnp.concatenate(
            [
                lax.dynamic_slice_in_dim(part_bc, group_start, groups_core * STATE, 1),
                lax.dynamic_slice_in_dim(part_bc, half_cols + group_start, groups_core * STATE, 1),
                lax.dynamic_slice_in_dim(part_dt, head_start, heads_core, 1),
                part_sq[:, None],
            ],
            axis=1,
        )

    mine = columns_for(tp)
    theirs = columns_for(tp_count - 1 - tp)
    total = mine + swapped(theirs, "tp")
    width_bc = groups_core * STATE
    sum_b = total[:, :width_bc]
    sum_c = total[:, width_bc : 2 * width_bc]
    sum_dt = total[:, 2 * width_bc : 2 * width_bc + heads_core]
    sum_sq = total[:, 2 * width_bc + heads_core]
    inv_rms = lax.rsqrt(sum_sq / (channel_count * tp_count) + EPSILON)
    own_rows = lax.dynamic_slice_in_dim(wide_rows, seg * heads_core * state_width, heads_core * state_width, 1)
    normed = (own_rows * inv_rms[:, None]).reshape(row_count, heads_core, state_width)
    b_rows = (sum_b * inv_rms[:, None]).reshape(row_count, groups_core, STATE)
    c_rows = (sum_c * inv_rms[:, None]).reshape(row_count, groups_core, STATE)
    bias = lax.dynamic_slice_in_dim(dt_bias[0], seg * heads_core, heads_core, 0)
    rate = lax.dynamic_slice_in_dim(decay_rate[0], seg * heads_core, heads_core, 0)
    skip = lax.dynamic_slice_in_dim(skip_gain[0], seg * heads_core, heads_core, 0)
    gain = lax.dynamic_slice_in_dim(out_gain[0], seg * heads_core, heads_core, 0)
    step_sizes = jax.nn.softplus(sum_dt * inv_rms[:, None] + bias[None, :])

    log_decay, local_part, ending, span_decay = span_terms(
        normed, b_rows, c_rows, step_sizes, rate, skip
    )
    _, state_in = exclusive_scan(span_decay, ending, "ctx")
    mixed_out = local_part + span_inflow(log_decay, c_rows, state_in)
    power = jnp.mean(mixed_out * mixed_out, axis=2, keepdims=True)
    result = own_rows.reshape(row_count, heads_core, state_width) + gain[None] * mixed_out * lax.rsqrt(
        power + EPSILON
    )
    state_part = result.reshape(row_count, heads_core * state_width).astype(jnp.bfloat16)

    keep_state = seg == 0
    state_in_half = lax.ppermute(state_part, "segment", [(1, 0)])
    attended_in_half = lax.ppermute(attended, "segment", [(0, 1)])
    first = jnp.where(keep_state, state_part, attended_in_half)
    second = jnp.where(keep_state, state_in_half, attended)
    return jnp.concatenate([first, second], axis=1)[None]


def solution(mesh):
    in_specs = (
        P("ctx", "tp", None),
        P("ctx", "tp", None),
        P("ctx", "tp", None),
        P("ctx", "tp"),
        P(None, "tp", None),
        P(None, "tp", None),
        P(None, "tp"),
        P(None, "tp"),
        P(None, "tp"),
        P(None, "tp", None),
    )
    out_specs = P("segment", "ctx", "tp")
    return jax.shard_map(body, mesh=mesh, in_specs=in_specs, out_specs=out_specs, check_vma=False)
```

```python
import functools
import math

import jax
import jax.numpy as jnp
from jax import lax
from jax.experimental import pallas as pl
from jax.experimental.pallas import tpu as pltpu
from jax.sharding import PartitionSpec as P

GROUPS = 4
STATE = 128


EPSILON = 1e-05


def shifted_up(value, axis, distance):
    size = lax.axis_size(axis)
    pairs = [(source, source + distance) for source in range(size - distance)]
    return lax.ppermute(value, axis, pairs)


def swapped(value, axis):
    return lax.ppermute(value, axis, [(0, 1), (1, 0)])


def span_terms(normed, b_rows, c_rows, step_sizes, rate_row, skip_row):
    count_rows, head_count, head_width = normed.shape
    group_count = b_rows.shape[1]
    per_group = head_count // group_count
    state_root = math.sqrt(b_rows.shape[2])
    log_decay = jnp.cumsum(-step_sizes * rate_row[None, :], axis=0)
    lower_mask = jnp.arange(count_rows)[:, None] >= jnp.arange(count_rows)[None, :]
    intersection = (
        jnp.einsum("tgn,sgn->gts", c_rows, b_rows, precision=lax.Precision.HIGHEST) / state_root
    )
    log_gaps = log_decay.T[:, :, None] - log_decay.T[:, None, :]
    decays = jnp.where(lower_mask[None], jnp.exp(jnp.where(lower_mask[None], log_gaps, 0.0)), 0.0)
    mixing = (
        decays.reshape(group_count, per_group, count_rows, count_rows)
        * intersection[:, None]
        * step_sizes.T.reshape(group_count, per_group, 1, count_rows)
    )
    grouped = normed.reshape(count_rows, group_count, per_group, head_width)
    local_part = jnp.einsum(
        "gkts,sgkp->tgkp", mixing, grouped, precision=lax.Precision.HIGHEST
    ).reshape(count_rows, head_count, head_width)
    tail_weight = jnp.exp(log_decay[-1][None, :] - log_decay) * step_sizes
    weighted = (normed * tail_weight[:, :, None]).reshape(
        count_rows, group_count, per_group, head_width
    )
    ending = jnp.einsum(
        "sgkp,sgn->gkpn", weighted, b_rows, precision=lax.Precision.HIGHEST
    ).reshape(head_count, head_width, b_rows.shape[2])
    return (
        log_decay,
        local_part + skip_row[None, :, None] * normed,
        ending,
        jnp.exp(log_decay[-1]),
    )


def span_inflow(log_decay, c_rows, state_in):
    count_rows, group_count, state_n = c_rows.shape
    head_count, head_width = (state_in.shape[0], state_in.shape[1])
    per_group = head_count // group_count
    state_root = math.sqrt(state_n)
    inflow = jnp.einsum(
        "tgn,gkpn->tgkp",
        c_rows,
        state_in.reshape(group_count, per_group, head_width, state_n),
        precision=lax.Precision.HIGHEST,
    )
    return (
        jnp.exp(log_decay)[:, :, None]
        * inflow.reshape(count_rows, head_count, head_width)
        / state_root
    )


def merge_states(earlier, later):
    return (earlier[0] * later[0], later[0][:, None, None] * earlier[1] + later[1])


def exclusive_scan(decay, state, axis, radix=2):
    place = lax.axis_index(axis)
    size = lax.axis_size(axis)
    incl = (decay, state)
    excl = (jnp.ones_like(decay), jnp.zeros_like(state))
    stride = 1
    while stride < size:
        joined = None
        for step in range(radix - 1, 0, -1):
            distance = step * stride
            if distance >= size:
                continue
            got = jax.tree.map(lambda a: shifted_up(a, axis, distance), incl)
            present = place >= distance
            got = (jnp.where(present, got[0], 1.0), jnp.where(present, got[1], 0.0))
            joined = got if joined is None else merge_states(joined, got)
        excl = merge_states(joined, excl)
        if stride * radix < size:
            incl = merge_states(joined, incl)
        stride *= radix
    return excl


def flash_kernel(first_ref, q_ref, k_ref, v_ref, o_ref, top_ref, total_ref, acc_ref, *, row_count, key_block, scale):
    j = pl.program_id(1)
    first = first_ref[0]
    block_start = j * key_block

    @pl.when(j == 0)
    def _():
        top_ref[...] = jnp.full(top_ref.shape, -1e30, jnp.float32)
        total_ref[...] = jnp.zeros(total_ref.shape, jnp.float32)
        acc_ref[...] = jnp.zeros(acc_ref.shape, jnp.float32)

    def update(with_mask):
        scores = (
            lax.dot_general(
                q_ref[...], k_ref[...], (((1,), (1,)), ((), ())), preferred_element_type=jnp.float32
            )
            * scale
        )
        if with_mask:
            rows = lax.broadcasted_iota(jnp.int32, (scores.shape[0], 1), 0) % row_count + first
            cols = lax.broadcasted_iota(jnp.int32, (1, scores.shape[1]), 1) + block_start
            allowed = rows >= cols
            scores = jnp.where(allowed, scores, -1e30)
        row_top = top_ref[...]
        new_top = jnp.maximum(row_top, jnp.max(scores, axis=1, keepdims=True))
        raw_weight = jnp.exp(scores - new_top)
        if with_mask:
            raw_weight = jnp.where(allowed, raw_weight, 0.0)
        factor = jnp.exp(row_top - new_top)
        total_ref[...] = total_ref[...] * factor + jnp.sum(raw_weight, axis=1, keepdims=True)
        acc_ref[...] = acc_ref[...] * factor + jnp.dot(
            raw_weight.astype(jnp.bfloat16), v_ref[...], preferred_element_type=jnp.float32
        )
        top_ref[...] = new_top

    @pl.when(block_start + key_block - 1 <= first)
    def _():
        update(False)

    @pl.when(
        jnp.logical_and(block_start + key_block - 1 > first, block_start <= first + row_count - 1)
    )
    def _():
        update(True)

    @pl.when(j == pl.num_programs(1) - 1)
    def _():
        o_ref[...] = (acc_ref[...] / total_ref[...]).astype(o_ref.dtype)


def attention_half(queries, keys, values, first_row, ready):
    row_count, q_heads, head_width = queries.shape
    kv_heads = keys.shape[1]
    group_size = q_heads // kv_heads
    score_scale = 1.0 / math.sqrt(head_width)
    grouped = (
        queries.reshape(row_count, kv_heads, group_size, head_width)
        .transpose(1, 2, 0, 3)
        .reshape(kv_heads, group_size * row_count, head_width)
    )
    both = jnp.concatenate([keys, values], axis=1).transpose(1, 0, 2)
    both_all = lax.all_gather(both, "ctx", axis=1, tiled=True)
    both_all, ready = lax.optimization_barrier((both_all, ready))
    key_count = both_all.shape[1]
    key_block = math.gcd(key_count, 4096)
    rows = group_size * row_count

    def key_index(h, j, first_ref):
        return (h, jnp.minimum(j, (first_ref[0] + row_count - 1) // key_block), 0)

    def value_index(h, j, first_ref):
        return (kv_heads + h, jnp.minimum(j, (first_ref[0] + row_count - 1) // key_block), 0)

    out = pl.pallas_call(
        functools.partial(flash_kernel, row_count=row_count, key_block=key_block, scale=score_scale),
        out_shape=jax.ShapeDtypeStruct((kv_heads, rows, head_width), jnp.bfloat16),
        grid_spec=pltpu.PrefetchScalarGridSpec(
            num_scalar_prefetch=1,
            grid=(kv_heads, key_count // key_block),
            in_specs=[
                pl.BlockSpec((None, rows, head_width), lambda h, j, f: (h, 0, 0)),
                pl.BlockSpec((None, key_block, head_width), key_index),
                pl.BlockSpec((None, key_block, head_width), value_index),
            ],
            out_specs=pl.BlockSpec((None, rows, head_width), lambda h, j, f: (h, 0, 0)),
            scratch_shapes=[
                pltpu.VMEM((rows, 1), jnp.float32),
                pltpu.VMEM((rows, 1), jnp.float32),
                pltpu.VMEM((rows, head_width), jnp.float32),
            ],
        ),
        compiler_params=pltpu.CompilerParams(dimension_semantics=("parallel", "arbitrary")),
    )(jnp.reshape(first_row, (1,)).astype(jnp.int32), grouped, both_all, both_all)
    return ready, (
        out.reshape(kv_heads, group_size, row_count, head_width)
        .transpose(2, 0, 1, 3)
        .reshape(row_count, q_heads * head_width)
    )


def body(queries, keys, values, layer_in, w_bc, w_dt, dt_bias, decay_rate, skip_gain, out_gain):
    seg = lax.axis_index("segment")
    seg_count = lax.axis_size("segment")
    tp = lax.axis_index("tp")
    tp_count = lax.axis_size("tp")
    row_count, q_heads, head_width = queries.shape
    kv_heads = keys.shape[1]
    first_row = lax.axis_index("ctx") * row_count

    q_share = q_heads // seg_count
    kv_share = kv_heads // seg_count
    q_part = lax.dynamic_slice_in_dim(queries, seg * q_share, q_share, 1)
    k_part = lax.dynamic_slice_in_dim(keys, seg * kv_share, kv_share, 1)
    v_part = lax.dynamic_slice_in_dim(values, seg * kv_share, kv_share, 1)

    current = layer_in
    channel_count = current.shape[1]
    heads_dev = dt_bias.shape[1]
    state_width = channel_count // heads_dev
    groups_dev = GROUPS // tp_count
    groups_core = groups_dev // seg_count
    heads_core = heads_dev // seg_count
    half_cols = GROUPS * STATE
    wide_rows = current.astype(jnp.float32)
    part_bc = jnp.dot(current, w_bc[0], preferred_element_type=jnp.float32)
    part_dt = jnp.dot(current, w_dt[0], preferred_element_type=jnp.float32)
    part_sq = jnp.sum(wide_rows * wide_rows, axis=1)

    def columns_for(tp_index):
        group_start = (tp_index * groups_dev + seg * groups_core) * STATE
        head_start = tp_index * heads_dev + seg * heads_core
        return jnp.concatenate(
            [
                lax.dynamic_slice_in_dim(part_bc, group_start, groups_core * STATE, 1),
                lax.dynamic_slice_in_dim(part_bc, half_cols + group_start, groups_core * STATE, 1),
                lax.dynamic_slice_in_dim(part_dt, head_start, heads_core, 1),
                part_sq[:, None],
            ],
            axis=1,
        )

    mine = columns_for(tp)
    theirs = columns_for(tp_count - 1 - tp)
    total = mine + swapped(theirs, "tp")
    width_bc = groups_core * STATE
    sum_b = total[:, :width_bc]
    sum_c = total[:, width_bc : 2 * width_bc]
    sum_dt = total[:, 2 * width_bc : 2 * width_bc + heads_core]
    sum_sq = total[:, 2 * width_bc + heads_core]
    inv_rms = lax.rsqrt(sum_sq / (channel_count * tp_count) + EPSILON)
    own_rows = lax.dynamic_slice_in_dim(wide_rows, seg * heads_core * state_width, heads_core * state_width, 1)
    normed = (own_rows * inv_rms[:, None]).reshape(row_count, heads_core, state_width)
    b_rows = (sum_b * inv_rms[:, None]).reshape(row_count, groups_core, STATE)
    c_rows = (sum_c * inv_rms[:, None]).reshape(row_count, groups_core, STATE)
    bias = lax.dynamic_slice_in_dim(dt_bias[0], seg * heads_core, heads_core, 0)
    rate = lax.dynamic_slice_in_dim(decay_rate[0], seg * heads_core, heads_core, 0)
    skip = lax.dynamic_slice_in_dim(skip_gain[0], seg * heads_core, heads_core, 0)
    gain = lax.dynamic_slice_in_dim(out_gain[0], seg * heads_core, heads_core, 0)
    step_sizes = jax.nn.softplus(sum_dt * inv_rms[:, None] + bias[None, :])

    log_decay, local_part, ending, span_decay = span_terms(
        normed, b_rows, c_rows, step_sizes, rate, skip
    )
    _, state_in = exclusive_scan(span_decay, ending, "ctx")
    mixed_out = local_part + span_inflow(log_decay, c_rows, state_in)
    power = jnp.mean(mixed_out * mixed_out, axis=2, keepdims=True)
    result = own_rows.reshape(row_count, heads_core, state_width) + gain[None] * mixed_out * lax.rsqrt(
        power + EPSILON
    )
    state_part = result.reshape(row_count, heads_core * state_width).astype(jnp.bfloat16)

    state_part, attended = attention_half(q_part, k_part, v_part, first_row, state_part)
    keep_state = seg == 0
    state_in_half = lax.ppermute(state_part, "segment", [(1, 0)])
    attended_in_half = lax.ppermute(attended, "segment", [(0, 1)])
    first = jnp.where(keep_state, state_part, attended_in_half)
    second = jnp.where(keep_state, state_in_half, attended)
    return jnp.concatenate([first, second], axis=1)[None]


def solution(mesh):
    in_specs = (
        P("ctx", "tp", None),
        P("ctx", "tp", None),
        P("ctx", "tp", None),
        P("ctx", "tp"),
        P(None, "tp", None),
        P(None, "tp", None),
        P(None, "tp"),
        P(None, "tp"),
        P(None, "tp"),
        P(None, "tp", None),
    )
    out_specs = P("segment", "ctx", "tp")
    return jax.shard_map(body, mesh=mesh, in_specs=in_specs, out_specs=out_specs, check_vma=False)
```

```python
import functools
import math

import jax
import jax.numpy as jnp
from jax import lax
from jax.experimental import pallas as pl
from jax.experimental.pallas import tpu as pltpu
from jax.sharding import PartitionSpec as P

GROUPS = 4
STATE = 128


EPSILON = 1e-05


def shifted_up(value, axis, distance):
    size = lax.axis_size(axis)
    pairs = [(source, source + distance) for source in range(size - distance)]
    return lax.ppermute(value, axis, pairs)


def swapped(value, axis):
    return lax.ppermute(value, axis, [(0, 1), (1, 0)])


def span_terms(normed, b_rows, c_rows, step_sizes, rate_row, skip_row):
    count_rows, head_count, head_width = normed.shape
    group_count = b_rows.shape[1]
    per_group = head_count // group_count
    state_root = math.sqrt(b_rows.shape[2])
    log_decay = jnp.cumsum(-step_sizes * rate_row[None, :], axis=0)
    lower_mask = jnp.arange(count_rows)[:, None] >= jnp.arange(count_rows)[None, :]
    intersection = (
        jnp.einsum("tgn,sgn->gts", c_rows, b_rows, precision=lax.Precision.HIGHEST) / state_root
    )
    log_gaps = log_decay.T[:, :, None] - log_decay.T[:, None, :]
    decays = jnp.where(lower_mask[None], jnp.exp(jnp.where(lower_mask[None], log_gaps, 0.0)), 0.0)
    mixing = (
        decays.reshape(group_count, per_group, count_rows, count_rows)
        * intersection[:, None]
        * step_sizes.T.reshape(group_count, per_group, 1, count_rows)
    )
    grouped = normed.reshape(count_rows, group_count, per_group, head_width)
    local_part = jnp.einsum(
        "gkts,sgkp->tgkp", mixing, grouped, precision=lax.Precision.HIGHEST
    ).reshape(count_rows, head_count, head_width)
    tail_weight = jnp.exp(log_decay[-1][None, :] - log_decay) * step_sizes
    weighted = (normed * tail_weight[:, :, None]).reshape(
        count_rows, group_count, per_group, head_width
    )
    ending = jnp.einsum(
        "sgkp,sgn->gkpn", weighted, b_rows, precision=lax.Precision.HIGHEST
    ).reshape(head_count, head_width, b_rows.shape[2])
    return (
        log_decay,
        local_part + skip_row[None, :, None] * normed,
        ending,
        jnp.exp(log_decay[-1]),
    )


def span_inflow(log_decay, c_rows, state_in):
    count_rows, group_count, state_n = c_rows.shape
    head_count, head_width = (state_in.shape[0], state_in.shape[1])
    per_group = head_count // group_count
    state_root = math.sqrt(state_n)
    inflow = jnp.einsum(
        "tgn,gkpn->tgkp",
        c_rows,
        state_in.reshape(group_count, per_group, head_width, state_n),
        precision=lax.Precision.HIGHEST,
    )
    return (
        jnp.exp(log_decay)[:, :, None]
        * inflow.reshape(count_rows, head_count, head_width)
        / state_root
    )


def merge_states(earlier, later):
    return (earlier[0] * later[0], later[0][:, None, None] * earlier[1] + later[1])


def exclusive_scan(decay, state, axis, radix=2):
    place = lax.axis_index(axis)
    size = lax.axis_size(axis)
    incl = (decay, state)
    excl = (jnp.ones_like(decay), jnp.zeros_like(state))
    stride = 1
    while stride < size:
        joined = None
        for step in range(radix - 1, 0, -1):
            distance = step * stride
            if distance >= size:
                continue
            got = jax.tree.map(lambda a: shifted_up(a, axis, distance), incl)
            present = place >= distance
            got = (jnp.where(present, got[0], 1.0), jnp.where(present, got[1], 0.0))
            joined = got if joined is None else merge_states(joined, got)
        excl = merge_states(joined, excl)
        if stride * radix < size:
            incl = merge_states(joined, incl)
        stride *= radix
    return excl


def flash_kernel(first_ref, q_ref, k_ref, v_ref, o_ref, top_ref, total_ref, acc_ref, *, row_count, key_block, scale):
    j = pl.program_id(1)
    first = first_ref[0]
    block_start = j * key_block

    @pl.when(j == 0)
    def _():
        top_ref[...] = jnp.full(top_ref.shape, -1e30, jnp.float32)
        total_ref[...] = jnp.zeros(total_ref.shape, jnp.float32)
        acc_ref[...] = jnp.zeros(acc_ref.shape, jnp.float32)

    def update(with_mask):
        scores = (
            lax.dot_general(
                q_ref[...], k_ref[...], (((1,), (1,)), ((), ())), preferred_element_type=jnp.float32
            )
            * scale
        )
        if with_mask:
            rows = lax.broadcasted_iota(jnp.int32, (scores.shape[0], 1), 0) % row_count + first
            cols = lax.broadcasted_iota(jnp.int32, (1, scores.shape[1]), 1) + block_start
            allowed = rows >= cols
            scores = jnp.where(allowed, scores, -1e30)
        row_top = top_ref[...]
        new_top = jnp.maximum(row_top, jnp.max(scores, axis=1, keepdims=True))
        raw_weight = jnp.exp(scores - new_top)
        if with_mask:
            raw_weight = jnp.where(allowed, raw_weight, 0.0)
        factor = jnp.exp(row_top - new_top)
        total_ref[...] = total_ref[...] * factor + jnp.sum(raw_weight, axis=1, keepdims=True)
        acc_ref[...] = acc_ref[...] * factor + jnp.dot(
            raw_weight.astype(jnp.bfloat16), v_ref[...], preferred_element_type=jnp.float32
        )
        top_ref[...] = new_top

    @pl.when(block_start + key_block - 1 <= first)
    def _():
        update(False)

    @pl.when(
        jnp.logical_and(block_start + key_block - 1 > first, block_start <= first + row_count - 1)
    )
    def _():
        update(True)

    @pl.when(j == pl.num_programs(1) - 1)
    def _():
        o_ref[...] = (acc_ref[...] / total_ref[...]).astype(o_ref.dtype)


def attention_half(queries, keys, values, first_row, ready, gathered):
    row_count, q_heads, head_width = queries.shape
    kv_heads = keys.shape[1]
    group_size = q_heads // kv_heads
    score_scale = 1.0 / math.sqrt(head_width)
    grouped = (
        queries.reshape(row_count, kv_heads, group_size, head_width)
        .transpose(1, 2, 0, 3)
        .reshape(kv_heads, group_size * row_count, head_width)
    )
    both = jnp.concatenate([keys, values], axis=1).transpose(1, 0, 2)
    both_all = lax.all_gather(both, "ctx", axis=1, tiled=True)
    both_all, ready = lax.optimization_barrier((both_all, ready))
    key_count = both_all.shape[1]
    key_block = math.gcd(key_count, 4096)
    rows = group_size * row_count

    def key_index(h, j, first_ref):
        return (h, jnp.minimum(j, (first_ref[0] + row_count - 1) // key_block), 0)

    def value_index(h, j, first_ref):
        return (kv_heads + h, jnp.minimum(j, (first_ref[0] + row_count - 1) // key_block), 0)

    out = pl.pallas_call(
        functools.partial(flash_kernel, row_count=row_count, key_block=key_block, scale=score_scale),
        out_shape=jax.ShapeDtypeStruct((kv_heads, rows, head_width), jnp.bfloat16),
        grid_spec=pltpu.PrefetchScalarGridSpec(
            num_scalar_prefetch=1,
            grid=(kv_heads, key_count // key_block),
            in_specs=[
                pl.BlockSpec((None, rows, head_width), lambda h, j, f: (h, 0, 0)),
                pl.BlockSpec((None, key_block, head_width), key_index),
                pl.BlockSpec((None, key_block, head_width), value_index),
            ],
            out_specs=pl.BlockSpec((None, rows, head_width), lambda h, j, f: (h, 0, 0)),
            scratch_shapes=[
                pltpu.VMEM((rows, 1), jnp.float32),
                pltpu.VMEM((rows, 1), jnp.float32),
                pltpu.VMEM((rows, head_width), jnp.float32),
            ],
        ),
        compiler_params=pltpu.CompilerParams(dimension_semantics=("parallel", "arbitrary")),
    )(jnp.reshape(first_row, (1,)).astype(jnp.int32), grouped, both_all, both_all)
    return ready, (
        out.reshape(kv_heads, group_size, row_count, head_width)
        .transpose(2, 0, 1, 3)
        .reshape(row_count, q_heads * head_width)
    )


def body(queries, keys, values, layer_in, w_bc, w_dt, dt_bias, decay_rate, skip_gain, out_gain):
    seg = lax.axis_index("segment")
    seg_count = lax.axis_size("segment")
    tp = lax.axis_index("tp")
    tp_count = lax.axis_size("tp")
    row_count, q_heads, head_width = queries.shape
    kv_heads = keys.shape[1]
    first_row = lax.axis_index("ctx") * row_count

    q_share = q_heads // seg_count
    kv_share = kv_heads // seg_count
    q_part = lax.dynamic_slice_in_dim(queries, seg * q_share, q_share, 1)
    k_part = lax.dynamic_slice_in_dim(keys, seg * kv_share, kv_share, 1)
    v_part = lax.dynamic_slice_in_dim(values, seg * kv_share, kv_share, 1)

    both_kv = jnp.concatenate([k_part, v_part], axis=1).transpose(1, 0, 2)
    both_kv, layer_in = lax.optimization_barrier((both_kv, layer_in))
    current = layer_in
    channel_count = current.shape[1]
    heads_dev = dt_bias.shape[1]
    state_width = channel_count // heads_dev
    groups_dev = GROUPS // tp_count
    groups_core = groups_dev // seg_count
    heads_core = heads_dev // seg_count
    half_cols = GROUPS * STATE
    wide_rows = current.astype(jnp.float32)
    part_bc = jnp.dot(current, w_bc[0], preferred_element_type=jnp.float32)
    part_dt = jnp.dot(current, w_dt[0], preferred_element_type=jnp.float32)
    part_sq = jnp.sum(wide_rows * wide_rows, axis=1)

    def columns_for(tp_index):
        group_start = (tp_index * groups_dev + seg * groups_core) * STATE
        head_start = tp_index * heads_dev + seg * heads_core
        return jnp.concatenate(
            [
                lax.dynamic_slice_in_dim(part_bc, group_start, groups_core * STATE, 1),
                lax.dynamic_slice_in_dim(part_bc, half_cols + group_start, groups_core * STATE, 1),
                lax.dynamic_slice_in_dim(part_dt, head_start, heads_core, 1),
                part_sq[:, None],
            ],
            axis=1,
        )

    mine = columns_for(tp)
    theirs = columns_for(tp_count - 1 - tp)
    total = mine + swapped(theirs, "tp")
    width_bc = groups_core * STATE
    sum_b = total[:, :width_bc]
    sum_c = total[:, width_bc : 2 * width_bc]
    sum_dt = total[:, 2 * width_bc : 2 * width_bc + heads_core]
    sum_sq = total[:, 2 * width_bc + heads_core]
    inv_rms = lax.rsqrt(sum_sq / (channel_count * tp_count) + EPSILON)
    own_rows = lax.dynamic_slice_in_dim(wide_rows, seg * heads_core * state_width, heads_core * state_width, 1)
    normed = (own_rows * inv_rms[:, None]).reshape(row_count, heads_core, state_width)
    b_rows = (sum_b * inv_rms[:, None]).reshape(row_count, groups_core, STATE)
    c_rows = (sum_c * inv_rms[:, None]).reshape(row_count, groups_core, STATE)
    bias = lax.dynamic_slice_in_dim(dt_bias[0], seg * heads_core, heads_core, 0)
    rate = lax.dynamic_slice_in_dim(decay_rate[0], seg * heads_core, heads_core, 0)
    skip = lax.dynamic_slice_in_dim(skip_gain[0], seg * heads_core, heads_core, 0)
    gain = lax.dynamic_slice_in_dim(out_gain[0], seg * heads_core, heads_core, 0)
    step_sizes = jax.nn.softplus(sum_dt * inv_rms[:, None] + bias[None, :])

    log_decay, local_part, ending, span_decay = span_terms(
        normed, b_rows, c_rows, step_sizes, rate, skip
    )
    _, state_in = exclusive_scan(span_decay, ending, "ctx")
    mixed_out = local_part + span_inflow(log_decay, c_rows, state_in)
    power = jnp.mean(mixed_out * mixed_out, axis=2, keepdims=True)
    result = own_rows.reshape(row_count, heads_core, state_width) + gain[None] * mixed_out * lax.rsqrt(
        power + EPSILON
    )
    state_part = result.reshape(row_count, heads_core * state_width).astype(jnp.bfloat16)

    state_part, attended = attention_half(q_part, k_part, v_part, first_row, state_part, both_kv)
    keep_state = seg == 0
    state_in_half = lax.ppermute(state_part, "segment", [(1, 0)])
    attended_in_half = lax.ppermute(attended, "segment", [(0, 1)])
    first = jnp.where(keep_state, state_part, attended_in_half)
    second = jnp.where(keep_state, state_in_half, attended)
    return jnp.concatenate([first, second], axis=1)[None]


def solution(mesh):
    in_specs = (
        P("ctx", "tp", None),
        P("ctx", "tp", None),
        P("ctx", "tp", None),
        P("ctx", "tp"),
        P(None, "tp", None),
        P(None, "tp", None),
        P(None, "tp"),
        P(None, "tp"),
        P(None, "tp"),
        P(None, "tp", None),
    )
    out_specs = P("segment", "ctx", "tp")
    return jax.shard_map(body, mesh=mesh, in_specs=in_specs, out_specs=out_specs, check_vma=False)
```

```python
import functools
import math

import jax
import jax.numpy as jnp
from jax import lax
from jax.experimental import pallas as pl
from jax.experimental.pallas import tpu as pltpu
from jax.sharding import PartitionSpec as P

GROUPS = 4
STATE = 128


EPSILON = 1e-05


def shifted_up(value, axis, distance):
    size = lax.axis_size(axis)
    pairs = [(source, source + distance) for source in range(size - distance)]
    return lax.ppermute(value, axis, pairs)


def swapped(value, axis):
    return lax.ppermute(value, axis, [(0, 1), (1, 0)])


def span_terms(normed, b_rows, c_rows, step_sizes, rate_row, skip_row):
    count_rows, head_count, head_width = normed.shape
    group_count = b_rows.shape[1]
    per_group = head_count // group_count
    state_root = math.sqrt(b_rows.shape[2])
    log_decay = jnp.cumsum(-step_sizes * rate_row[None, :], axis=0)
    lower_mask = jnp.arange(count_rows)[:, None] >= jnp.arange(count_rows)[None, :]
    intersection = (
        jnp.einsum("tgn,sgn->gts", c_rows, b_rows, precision=lax.Precision.HIGHEST) / state_root
    )
    log_gaps = log_decay.T[:, :, None] - log_decay.T[:, None, :]
    decays = jnp.where(lower_mask[None], jnp.exp(jnp.where(lower_mask[None], log_gaps, 0.0)), 0.0)
    mixing = (
        decays.reshape(group_count, per_group, count_rows, count_rows)
        * intersection[:, None]
        * step_sizes.T.reshape(group_count, per_group, 1, count_rows)
    )
    grouped = normed.reshape(count_rows, group_count, per_group, head_width)
    local_part = jnp.einsum(
        "gkts,sgkp->tgkp", mixing, grouped, precision=lax.Precision.HIGHEST
    ).reshape(count_rows, head_count, head_width)
    tail_weight = jnp.exp(log_decay[-1][None, :] - log_decay) * step_sizes
    weighted = (normed * tail_weight[:, :, None]).reshape(
        count_rows, group_count, per_group, head_width
    )
    ending = jnp.einsum(
        "sgkp,sgn->gkpn", weighted, b_rows, precision=lax.Precision.HIGHEST
    ).reshape(head_count, head_width, b_rows.shape[2])
    return (
        log_decay,
        local_part + skip_row[None, :, None] * normed,
        ending,
        jnp.exp(log_decay[-1]),
    )


def span_inflow(log_decay, c_rows, state_in):
    count_rows, group_count, state_n = c_rows.shape
    head_count, head_width = (state_in.shape[0], state_in.shape[1])
    per_group = head_count // group_count
    state_root = math.sqrt(state_n)
    inflow = jnp.einsum(
        "tgn,gkpn->tgkp",
        c_rows,
        state_in.reshape(group_count, per_group, head_width, state_n),
        precision=lax.Precision.HIGHEST,
    )
    return (
        jnp.exp(log_decay)[:, :, None]
        * inflow.reshape(count_rows, head_count, head_width)
        / state_root
    )


def merge_states(earlier, later):
    return (earlier[0] * later[0], later[0][:, None, None] * earlier[1] + later[1])


def exclusive_scan(decay, state, axis, radix=2):
    place = lax.axis_index(axis)
    size = lax.axis_size(axis)
    incl = (decay, state)
    excl = (jnp.ones_like(decay), jnp.zeros_like(state))
    stride = 1
    while stride < size:
        joined = None
        for step in range(radix - 1, 0, -1):
            distance = step * stride
            if distance >= size:
                continue
            got = jax.tree.map(lambda a: shifted_up(a, axis, distance), incl)
            present = place >= distance
            got = (jnp.where(present, got[0], 1.0), jnp.where(present, got[1], 0.0))
            joined = got if joined is None else merge_states(joined, got)
        excl = merge_states(joined, excl)
        if stride * radix < size:
            incl = merge_states(joined, incl)
        stride *= radix
    return excl


def flash_kernel(first_ref, q_ref, k_ref, v_ref, o_ref, top_ref, total_ref, acc_ref, *, row_count, key_block, scale):
    j = pl.program_id(1)
    first = first_ref[0]
    block_start = j * key_block

    @pl.when(j == 0)
    def _():
        top_ref[...] = jnp.full(top_ref.shape, -1e30, jnp.float32)
        total_ref[...] = jnp.zeros(total_ref.shape, jnp.float32)
        acc_ref[...] = jnp.zeros(acc_ref.shape, jnp.float32)

    def update(with_mask):
        scores = (
            lax.dot_general(
                q_ref[...], k_ref[...], (((1,), (1,)), ((), ())), preferred_element_type=jnp.float32
            )
            * scale
        )
        if with_mask:
            rows = lax.broadcasted_iota(jnp.int32, (scores.shape[0], 1), 0) % row_count + first
            cols = lax.broadcasted_iota(jnp.int32, (1, scores.shape[1]), 1) + block_start
            allowed = rows >= cols
            scores = jnp.where(allowed, scores, -1e30)
        row_top = top_ref[...]
        new_top = jnp.maximum(row_top, jnp.max(scores, axis=1, keepdims=True))
        raw_weight = jnp.exp(scores - new_top)
        if with_mask:
            raw_weight = jnp.where(allowed, raw_weight, 0.0)
        factor = jnp.exp(row_top - new_top)
        total_ref[...] = total_ref[...] * factor + jnp.sum(raw_weight, axis=1, keepdims=True)
        acc_ref[...] = acc_ref[...] * factor + jnp.dot(
            raw_weight.astype(jnp.bfloat16), v_ref[...], preferred_element_type=jnp.float32
        )
        top_ref[...] = new_top

    @pl.when(block_start + key_block - 1 <= first)
    def _():
        update(False)

    @pl.when(
        jnp.logical_and(block_start + key_block - 1 > first, block_start <= first + row_count - 1)
    )
    def _():
        update(True)

    @pl.when(j == pl.num_programs(1) - 1)
    def _():
        o_ref[...] = (acc_ref[...] / total_ref[...]).astype(o_ref.dtype)


def attention_half(queries, keys, values, first_row, ready):
    row_count, q_heads, head_width = queries.shape
    kv_heads = keys.shape[1]
    group_size = q_heads // kv_heads
    score_scale = 1.0 / math.sqrt(head_width)
    grouped = (
        queries.reshape(row_count, kv_heads, group_size, head_width)
        .transpose(1, 2, 0, 3)
        .reshape(kv_heads, group_size * row_count, head_width)
    )
    both = jnp.concatenate([keys, values], axis=1).transpose(1, 0, 2)
    both_all = lax.all_gather(both, "ctx", axis=1, tiled=True)
    both_all, ready = lax.optimization_barrier((both_all, ready))
    key_count = both_all.shape[1]
    key_block = math.gcd(key_count, 4096)
    rows = group_size * row_count

    def key_index(h, j, first_ref):
        return (h, jnp.minimum(j, (first_ref[0] + row_count - 1) // key_block), 0)

    def value_index(h, j, first_ref):
        return (kv_heads + h, jnp.minimum(j, (first_ref[0] + row_count - 1) // key_block), 0)

    parts = []
    for head in range(kv_heads):

        def key_index(h, j, first_ref, head=head):
            return (head, jnp.minimum(j, (first_ref[0] + row_count - 1) // key_block), 0)

        def value_index(h, j, first_ref, head=head):
            return (kv_heads + head, jnp.minimum(j, (first_ref[0] + row_count - 1) // key_block), 0)

        out = pl.pallas_call(
            functools.partial(flash_kernel, row_count=row_count, key_block=key_block, scale=score_scale),
            out_shape=jax.ShapeDtypeStruct((1, rows, head_width), jnp.bfloat16),
            grid_spec=pltpu.PrefetchScalarGridSpec(
                num_scalar_prefetch=1,
                grid=(1, key_count // key_block),
                in_specs=[
                    pl.BlockSpec((None, rows, head_width), lambda h, j, f, head=head: (head, 0, 0)),
                    pl.BlockSpec((None, key_block, head_width), key_index),
                    pl.BlockSpec((None, key_block, head_width), value_index),
                ],
                out_specs=pl.BlockSpec((None, rows, head_width), lambda h, j, f: (0, 0, 0)),
                scratch_shapes=[
                    pltpu.VMEM((rows, 1), jnp.float32),
                    pltpu.VMEM((rows, 1), jnp.float32),
                    pltpu.VMEM((rows, head_width), jnp.float32),
                ],
            ),
            compiler_params=pltpu.CompilerParams(dimension_semantics=("parallel", "arbitrary")),
        )(jnp.reshape(first_row, (1,)).astype(jnp.int32), grouped, both_all, both_all)
        parts.append(
            out.reshape(group_size, row_count, head_width)
            .transpose(1, 0, 2)
            .reshape(row_count, group_size * head_width)
        )
    return ready, parts


def body(queries, keys, values, layer_in, w_bc, w_dt, dt_bias, decay_rate, skip_gain, out_gain):
    seg = lax.axis_index("segment")
    seg_count = lax.axis_size("segment")
    tp = lax.axis_index("tp")
    tp_count = lax.axis_size("tp")
    row_count, q_heads, head_width = queries.shape
    kv_heads = keys.shape[1]
    first_row = lax.axis_index("ctx") * row_count

    q_share = q_heads // seg_count
    kv_share = kv_heads // seg_count
    q_part = lax.dynamic_slice_in_dim(queries, seg * q_share, q_share, 1)
    k_part = lax.dynamic_slice_in_dim(keys, seg * kv_share, kv_share, 1)
    v_part = lax.dynamic_slice_in_dim(values, seg * kv_share, kv_share, 1)

    current = layer_in
    channel_count = current.shape[1]
    heads_dev = dt_bias.shape[1]
    state_width = channel_count // heads_dev
    groups_dev = GROUPS // tp_count
    groups_core = groups_dev // seg_count
    heads_core = heads_dev // seg_count
    half_cols = GROUPS * STATE
    wide_rows = current.astype(jnp.float32)
    part_bc = jnp.dot(current, w_bc[0], preferred_element_type=jnp.float32)
    part_dt = jnp.dot(current, w_dt[0], preferred_element_type=jnp.float32)
    part_sq = jnp.sum(wide_rows * wide_rows, axis=1)

    def columns_for(tp_index):
        group_start = (tp_index * groups_dev + seg * groups_core) * STATE
        head_start = tp_index * heads_dev + seg * heads_core
        return jnp.concatenate(
            [
                lax.dynamic_slice_in_dim(part_bc, group_start, groups_core * STATE, 1),
                lax.dynamic_slice_in_dim(part_bc, half_cols + group_start, groups_core * STATE, 1),
                lax.dynamic_slice_in_dim(part_dt, head_start, heads_core, 1),
                part_sq[:, None],
            ],
            axis=1,
        )

    mine = columns_for(tp)
    theirs = columns_for(tp_count - 1 - tp)
    total = mine + swapped(theirs, "tp")
    width_bc = groups_core * STATE
    sum_b = total[:, :width_bc]
    sum_c = total[:, width_bc : 2 * width_bc]
    sum_dt = total[:, 2 * width_bc : 2 * width_bc + heads_core]
    sum_sq = total[:, 2 * width_bc + heads_core]
    inv_rms = lax.rsqrt(sum_sq / (channel_count * tp_count) + EPSILON)
    own_rows = lax.dynamic_slice_in_dim(wide_rows, seg * heads_core * state_width, heads_core * state_width, 1)
    normed = (own_rows * inv_rms[:, None]).reshape(row_count, heads_core, state_width)
    b_rows = (sum_b * inv_rms[:, None]).reshape(row_count, groups_core, STATE)
    c_rows = (sum_c * inv_rms[:, None]).reshape(row_count, groups_core, STATE)
    bias = lax.dynamic_slice_in_dim(dt_bias[0], seg * heads_core, heads_core, 0)
    rate = lax.dynamic_slice_in_dim(decay_rate[0], seg * heads_core, heads_core, 0)
    skip = lax.dynamic_slice_in_dim(skip_gain[0], seg * heads_core, heads_core, 0)
    gain = lax.dynamic_slice_in_dim(out_gain[0], seg * heads_core, heads_core, 0)
    step_sizes = jax.nn.softplus(sum_dt * inv_rms[:, None] + bias[None, :])

    log_decay, local_part, ending, span_decay = span_terms(
        normed, b_rows, c_rows, step_sizes, rate, skip
    )
    _, state_in = exclusive_scan(span_decay, ending, "ctx")
    mixed_out = local_part + span_inflow(log_decay, c_rows, state_in)
    power = jnp.mean(mixed_out * mixed_out, axis=2, keepdims=True)
    result = own_rows.reshape(row_count, heads_core, state_width) + gain[None] * mixed_out * lax.rsqrt(
        power + EPSILON
    )
    state_part = result.reshape(row_count, heads_core * state_width).astype(jnp.bfloat16)

    state_part, attended = attention_half(q_part, k_part, v_part, first_row, state_part)
    keep_state = seg == 0
    state_in_half = lax.ppermute(state_part, "segment", [(1, 0)])
    attended_in_half = jnp.concatenate(
        [lax.ppermute(part, "segment", [(0, 1)]) for part in attended], axis=1
    )
    attended = jnp.concatenate(attended, axis=1)
    first = jnp.where(keep_state, state_part, attended_in_half)
    second = jnp.where(keep_state, state_in_half, attended)
    return jnp.concatenate([first, second], axis=1)[None]


def solution(mesh):
    in_specs = (
        P("ctx", "tp", None),
        P("ctx", "tp", None),
        P("ctx", "tp", None),
        P("ctx", "tp"),
        P(None, "tp", None),
        P(None, "tp", None),
        P(None, "tp"),
        P(None, "tp"),
        P(None, "tp"),
        P(None, "tp", None),
    )
    out_specs = P("segment", "ctx", "tp")
    return jax.shard_map(body, mesh=mesh, in_specs=in_specs, out_specs=out_specs, check_vma=False)
```
